256 devices in a mesh: au: 4 (over x), vert: 8 (over z), af: 8 (over y, core).
Axes of the slice: x: 4, y: 4, z: 8, core: 2. Of those that a mesh axis runs over, the one named last changes fastest.
Arguments:
- visib: float32 [8, 512, 1024], P('af', ('au', 'vert')), may hold values from -6 to 6
- coords: float32 [8, 512, 1024], P('af', ('au', 'vert')), may hold values from -16 to 16
- owner: int32 [8, 512], P('af', ('au', 'vert')), may hold values from 0 to 31, as said below
- offsets: int32 [8, 512, 2], P('af', ('au', 'vert')), may hold values from 0 to 448
- stations: int32 [8, 512, 2], P('af', ('au', 'vert')), may hold values from 0 to 511, as said below
- live: int32 [8, 32], P('af', ('au', 'vert')), may hold values from 16 to 16, as said below
- beams: bfloat16 [8, 512, 8192], P('af', ('au', 'vert')), may hold values from -4.1875 to 4.1875
- taper: float32 [2048, 4096], P('au', 'vert'), may hold values from 0.5 to 2
Outputs:
- predicted: float32 [8, 512, 1024], P('af', ('au', 'vert'))
- model_grid: float32 [2, 2048, 4096], P(None, 'au', 'vert')
The draws below stay inside these ranges and needn't reach their ends.
Inputs may be any that keep to these rules, and one draw needn't show every extreme that they name: A tile id is tile row times the number of tile columns plus tile column. The owner of a live block is its holder's tile or one of the eight tiles around it inside the grid; the owner of a dead block is its holder's tile. Among the live blocks of one holder, at most 2 name any one other tile, and in every channel group one tile receives exactly 2 blocks from each of its eight neighbours. The two stations of a block differ. Counting both stations of all 16 blocks of one holder, at most 3 of these entries lie on the stations s of any one value of s // 16, and some value takes exactly 3 on every holder. In every channel group some holder has all 16 blocks live.
All inputs are finite; a program needn't handle non-finite values.
Results may differ from the reference program's by a relative error of at most 0.0004.
Values may be sent and summed in bfloat16 or wider, within the bound.
No kernel may reach another device: no remote copies, remote signals or barrier semaphores. Data moves between devices by JAX's collectives and lax.ppermute only.
A program may use at most 64 MiB of HBM per device.

```python
import math
import jax
import jax.numpy as jnp
from jax import lax

S = 64
STATIONS = 512
ROWS = 512
CAP = 2
NB = 16
TS = 512
NGRP = 8
BLOCKS = 512
NU = 2048
NV = 4096
N_AU = 4
N_VERT = 8


def block_plan(key):
    tile_total = N_AU * N_VERT
    base_key = jax.random.fold_in(key, 11)
    key_live, key_full, key_row, key_col, key_count, key_order = jax.random.split(base_key, 6)
    live_count = jax.random.randint(key_live, (NGRP, tile_total), 8 * CAP, NB + 1)
    fullest = jax.random.randint(key_full, (NGRP, 1), 0, tile_total)
    tile_ids = jnp.arange(tile_total, dtype=jnp.int32)
    live_count = jnp.where(tile_ids[None, :] == fullest, NB, live_count)
    busy_row = jax.random.randint(key_row, (NGRP, 1, 1), 1, N_AU - 1)
    busy_col = jax.random.randint(key_col, (NGRP, 1, 1), 1, N_VERT - 1)
    route_ids = jnp.arange(9, dtype=jnp.int32)
    step_row = route_ids // 3 - 1
    step_col = route_ids % 3 - 1
    dest_row = (tile_ids // N_VERT)[None, :, None] + step_row[None, None, :]
    dest_col = (tile_ids % N_VERT)[None, :, None] + step_col[None, None, :]
    inside = (dest_row >= 0) & (dest_row < N_AU) & (dest_col >= 0) & (dest_col < N_VERT) & (route_ids != 4)[None, None, :]
    counts = jax.random.randint(key_count, (NGRP, tile_total, 9), 0, CAP + 1)
    is_busy = (dest_row == busy_row) & (dest_col == busy_col)
    counts = jnp.where(is_busy, CAP, counts)
    counts = jnp.where(inside, counts, 0)
    ends_at = jnp.cumsum(counts, axis=2)
    sequence = jnp.arange(NB, dtype=jnp.int32)
    seq_route = jnp.sum((ends_at[:, :, None, :] <= sequence[None, None, :, None]).astype(jnp.int32), axis=3)
    seq_route = jnp.where(seq_route >= 9, 4, seq_route)
    scores = jax.random.randint(key_order, (NGRP, tile_total, NB), 0, 1 << 20)
    scores = jnp.where(sequence[None, None, :] < live_count[:, :, None], scores, (1 << 20) + sequence[None, None, :])
    scores = scores * NB + sequence[None, None, :]
    order_of = jnp.argsort(scores, axis=2, stable=True)
    inverse = jnp.argsort(order_of, axis=2, stable=True)
    block_route = jnp.take_along_axis(seq_route, inverse, axis=2)
    own_row = (tile_ids // N_VERT)[None, :, None] + block_route // 3 - 1
    own_col = (tile_ids % N_VERT)[None, :, None] + block_route % 3 - 1
    owner_ids = own_row * N_VERT + own_col
    return (live_count.astype(jnp.int32), owner_ids.reshape(NGRP, tile_total * NB).astype(jnp.int32))


def draw_live(key, part):
    return block_plan(key)[0]


def draw_owner(key, part):
    return block_plan(key)[1]


def draw_stations(key, part):
    tile_total = N_AU * N_VERT
    ask_total = 2 * NB
    per_dev = STATIONS // tile_total
    ask_cap = ask_total // tile_total + 2
    full_most = ask_total // ask_cap
    base_key = jax.random.fold_in(key, 23)
    key_full, key_owner, key_shuffle, key_local = jax.random.split(base_key, 4)
    full_groups = jax.random.randint(key_full, (NGRP, tile_total, 1), 1, full_most + 1)
    ask_index = jnp.arange(ask_total, dtype=jnp.int32)[None, None, :]
    slot_group = jnp.where(ask_index < full_groups * ask_cap, ask_index // ask_cap, full_groups + (ask_index - full_groups * ask_cap) % (tile_total - full_groups))
    owner_scores = jax.random.randint(key_owner, (NGRP, tile_total, tile_total), 0, 1 << 20) * tile_total + jnp.arange(tile_total, dtype=jnp.int32)
    owner_perm = jnp.argsort(owner_scores, axis=2, stable=True).astype(jnp.int32)
    keeper = jnp.take_along_axis(owner_perm, slot_group, axis=2)
    ask_scores = jax.random.randint(key_shuffle, (NGRP, tile_total, ask_total), 0, 1 << 20) * ask_total + jnp.arange(ask_total, dtype=jnp.int32)
    shuffle = jnp.argsort(ask_scores, axis=2, stable=True)
    keeper = jnp.take_along_axis(keeper, shuffle, axis=2).reshape(NGRP, tile_total, NB, 2)
    local_id = jax.random.randint(key_local, (NGRP, tile_total, ask_total), 0, per_dev).reshape(NGRP, tile_total, NB, 2)
    first = keeper[..., 0] * per_dev + local_id[..., 0]
    clash = (keeper[..., 0] == keeper[..., 1]) & (local_id[..., 0] == local_id[..., 1])
    second_local = jnp.where(clash, (local_id[..., 1] + 1) % per_dev, local_id[..., 1])
    second = keeper[..., 1] * per_dev + second_local
    return jnp.stack([first, second], axis=-1).reshape(NGRP, tile_total * NB, 2).astype(jnp.int32)


def plant(values, rng, low, high):
    longest = values.shape.index(max(values.shape))
    spots = []
    for shift in (0, 1):
        where = [jax.random.randint(jax.random.fold_in(rng, axis), (), 0, length) for axis, length in enumerate(values.shape)]
        where[longest] = (where[longest] + shift) % values.shape[longest]
        spots.append(tuple(where))
    return values.at[spots[0]].set(low).at[spots[1]].set(high)


def level_of(key, shape, shards, smallest, largest):
    factor_of, own = 1.0, jax.random.fold_in(key, 6)
    for dim, blocks in shards:
        draws = jnp.exp(jax.random.uniform(jax.random.fold_in(own, dim), (blocks,), jnp.float32, smallest / len(shards), largest / len(shards)))
        factor_of = factor_of * jnp.repeat(draws, shape[dim] // blocks).reshape([-1 if axis == dim else 1 for axis in range(len(shape))])
    return factor_of


def gaussian(rng, dims, width, most, cuts=(), kind=jnp.bfloat16):
    values = jax.random.normal(rng, dims, jnp.float32) * width
    if len(cuts) > 0:
        values = level_of(rng, dims, cuts, -0.22, 0.18) * values
    return jnp.clip(values, min=-most, max=most).astype(kind)


def setup_inputs(seed: int = 0) -> dict:
    arg_keys = jax.random.split(jax.random.key(seed), 9)
    visib = gaussian(arg_keys[0], (NGRP, BLOCKS, 2 * ROWS), 1.0, 6.0, ((0, 8), (1, 32)), jnp.float32)
    coords = jnp.clip(jax.random.uniform(arg_keys[1], (NGRP, BLOCKS, 2 * ROWS), jnp.float32, -16.0, 16.0) * level_of(arg_keys[1], (NGRP, BLOCKS, 2 * ROWS), ((0, 8), (1, 32)), -0.4, 0.0), -16.0, 16.0)
    owner = draw_owner(jax.random.fold_in(arg_keys[8], 71), 0)
    offsets = plant(jax.random.randint(arg_keys[3], (NGRP, BLOCKS, 2), 0, TS - S + 1), jax.random.fold_in(arg_keys[3], 1), 0, TS - S).astype(jnp.int32)
    stations = draw_stations(jax.random.fold_in(arg_keys[8], 71), 0)
    live = draw_live(jax.random.fold_in(arg_keys[8], 71), 0)
    beams = gaussian(arg_keys[6], (NGRP, STATIONS, 2 * S * S), 0.7, 4.1875, ((0, 8), (1, 32)))
    taper = jnp.clip(jnp.exp(math.log(2.0) - 1.3862944 * jax.random.uniform(arg_keys[7], (NU, NV), jnp.float32) ** level_of(arg_keys[7], (NU, NV), ((0, 4), (1, 8)), -0.2, 0.2)), 0.5, 2.0)
    return dict(visib=visib, coords=coords, owner=owner, offsets=offsets, stations=stations, live=live, beams=beams, taper=taper)


highest = lax.Precision.HIGHEST

def tables(side_len):
    positions = jnp.arange(side_len, dtype=jnp.int32)
    wrapped = positions[:, None] * positions[None, :] % side_len
    angles = wrapped.astype(jnp.float32) * (2.0 * math.pi / side_len)
    scaling = 1.0 / math.sqrt(side_len)
    return (jnp.cos(angles) * scaling, -jnp.sin(angles) * scaling)

def rotate(values):
    half_width = values.shape[-1] // 2
    return jnp.concatenate([-values[..., half_width:], values[..., :half_width]], axis=-1)

def complex_mul(values, factor):
    half_width = values.shape[-1] // 2
    x_real, x_imag = (values[..., :half_width], values[..., half_width:])
    a_real, a_imag = (factor[..., :half_width], factor[..., half_width:])
    return jnp.concatenate([x_real * a_real - x_imag * a_imag, x_real * a_imag + x_imag * a_real], axis=-1)

def conj_mul(values, factor):
    half_width = values.shape[-1] // 2
    x_real, x_imag = (values[..., :half_width], values[..., half_width:])
    a_real, a_imag = (factor[..., :half_width], factor[..., half_width:])
    return jnp.concatenate([x_real * a_real + x_imag * a_imag, x_imag * a_real - x_real * a_imag], axis=-1)

def phases(coords_in, side_len):
    centre = jnp.arange(side_len, dtype=jnp.float32) - side_len / 2
    angles = coords_in[..., None] * centre * (2.0 * math.pi / side_len)
    return (jnp.cos(angles), jnp.sin(angles))

def grid_blocks(visib_rows, coord_rows, beam_terms):
    row_count = visib_rows.shape[-1] // 2
    side_len = beam_terms.shape[-2]
    cos_u, sin_u = phases(coord_rows[..., :row_count], side_len)
    cos_v, sin_v = phases(coord_rows[..., row_count:], side_len)
    vis_real = visib_rows[..., :row_count, None]
    vis_imag = visib_rows[..., row_count:, None]
    weighted = jnp.concatenate([vis_real * cos_v - vis_imag * sin_v, vis_real * sin_v + vis_imag * cos_v], axis=-1)
    first = jnp.einsum('krl,krc->klc', cos_u, weighted, precision=highest)
    second = jnp.einsum('krl,krc->klc', sin_u, weighted, precision=highest)
    image_part = (first + rotate(second)) * (1.0 / math.sqrt(row_count))
    image_part = complex_mul(image_part, beam_terms)
    table_real, table_imag = tables(side_len)
    left_side = jnp.einsum('al,klc->kac', table_real, image_part, precision=highest)
    left_side = left_side + rotate(jnp.einsum('al,klc->kac', table_imag, image_part, precision=highest))
    right_side = jnp.concatenate([jnp.concatenate([table_real, table_imag], 1), jnp.concatenate([-table_imag, table_real], 1)], 0)
    return jnp.einsum('kac,cd->kad', left_side, right_side, precision=highest)

def degrid_blocks(windows, coord_rows, beam_terms):
    side_len = windows.shape[-2]
    row_count = coord_rows.shape[-1] // 2
    table_real, table_imag = tables(side_len)
    left_side = jnp.einsum('al,klc->kac', table_real, windows, precision=highest)
    left_side = left_side - rotate(jnp.einsum('al,klc->kac', table_imag, windows, precision=highest))
    right_side = jnp.concatenate([jnp.concatenate([table_real, -table_imag], 1), jnp.concatenate([table_imag, table_real], 1)], 0)
    image_part = jnp.einsum('kac,cd->kad', left_side, right_side, precision=highest)
    image_part = conj_mul(image_part, beam_terms)
    cos_u, sin_u = phases(coord_rows[..., :row_count], side_len)
    cos_v, sin_v = phases(coord_rows[..., row_count:], side_len)
    first = jnp.einsum('krl,klc->krc', cos_u, image_part, precision=highest)
    second = jnp.einsum('krl,klc->krc', sin_u, image_part, precision=highest)
    along_rows = first - rotate(second)
    a_real = along_rows[..., :side_len]
    a_imag = along_rows[..., side_len:]
    real_part = lax.optimization_barrier(jnp.sum(a_real * cos_v + a_imag * sin_v, axis=-1))
    imag_part = lax.optimization_barrier(jnp.sum(a_imag * cos_v - a_real * sin_v, axis=-1))
    return jnp.concatenate([real_part, imag_part], axis=-1) * (1.0 / side_len)

def group_terms(beam_rows, pair_ids):
    block_total = pair_ids.shape[0]
    first = jnp.take(beam_rows, pair_ids[:, 0], axis=0).astype(jnp.float32).reshape(block_total, S, 2 * S)
    second = jnp.take(beam_rows, pair_ids[:, 1], axis=0).astype(jnp.float32).reshape(block_total, S, 2 * S)
    return conj_mul(first, second)

def reference(visib, coords, owner, offsets, stations, live, beams, taper):
    block_ids = jnp.arange(BLOCKS, dtype=jnp.int32)
    zero_index = jnp.zeros((), jnp.int32)

    def positions_of(group_id):
        tile_ids = owner[group_id].astype(jnp.int32)
        shifts_in = offsets[group_id].astype(jnp.int32)
        row_start = (tile_ids // N_VERT * TS + shifts_in[:, 0]).astype(jnp.int32)
        col_start = (tile_ids % N_VERT * TS + shifts_in[:, 1]).astype(jnp.int32)
        counts_in = live[group_id].astype(jnp.int32)
        is_alive = (block_ids % NB < counts_in[block_ids // NB]).astype(jnp.float32)
        return (row_start, col_start, is_alive)

    def add_group(group_id, summed_grid):
        row_start, col_start, is_alive = positions_of(group_id)
        beam_terms = group_terms(beams[group_id], stations[group_id])
        subgrids = grid_blocks(visib[group_id], coords[group_id], beam_terms) * is_alive[:, None, None]

        def add_one(block_at, partial_value):
            subgrid = subgrids[block_at].reshape(S, 2, S).transpose(1, 0, 2)
            corner = (zero_index, row_start[block_at], col_start[block_at])
            window = lax.dynamic_slice(partial_value, corner, (2, S, S))
            return lax.dynamic_update_slice(partial_value, window + subgrid, corner)
        return lax.fori_loop(0, BLOCKS, add_one, summed_grid)
    summed_grid = lax.fori_loop(0, NGRP, add_group, jnp.zeros((2, NU, NV), jnp.float32))
    model_grid = summed_grid * taper[None]

    def predict(group_id):
        row_start, col_start, is_alive = positions_of(group_id)
        beam_terms = group_terms(beams[group_id], stations[group_id])

        def cut_window(row_at, col_at):
            return lax.dynamic_slice(model_grid, (zero_index, row_at, col_at), (2, S, S))
        windows = jax.vmap(cut_window)(row_start, col_start)
        windows = jnp.transpose(windows, (0, 2, 1, 3)).reshape(BLOCKS, S, 2 * S)
        return degrid_blocks(windows, coords[group_id], beam_terms) * is_alive[:, None]
    predicted = lax.map(predict, jnp.arange(NGRP, dtype=jnp.int32))
    return (predicted, model_grid)
```

```python
import math

import jax
import jax.numpy as jnp
from jax import lax
from jax.sharding import PartitionSpec as P

S = 64
CAP = 2
NB = 16
TS = 512


highest = lax.Precision.HIGHEST


def shifted(value, axis, steps):
    count = lax.axis_size(axis)
    leading, last = (max(0, -steps), min(count, count - steps))
    return lax.ppermute(value, axis, [(source, source + steps) for source in range(leading, last)])


def tables(side_len):
    positions = jnp.arange(side_len, dtype=jnp.int32)
    wrapped = positions[:, None] * positions[None, :] % side_len
    angles = wrapped.astype(jnp.float32) * (2.0 * math.pi / side_len)
    scaling = 1.0 / math.sqrt(side_len)
    return (jnp.cos(angles) * scaling, -jnp.sin(angles) * scaling)


def rotate(values):
    half_width = values.shape[-1] // 2
    return jnp.concatenate([-values[..., half_width:], values[..., :half_width]], axis=-1)


def complex_mul(values, factor):
    half_width = values.shape[-1] // 2
    x_real, x_imag = (values[..., :half_width], values[..., half_width:])
    a_real, a_imag = (factor[..., :half_width], factor[..., half_width:])
    return jnp.concatenate(
        [x_real * a_real - x_imag * a_imag, x_real * a_imag + x_imag * a_real], axis=-1
    )


def conj_mul(values, factor):
    half_width = values.shape[-1] // 2
    x_real, x_imag = (values[..., :half_width], values[..., half_width:])
    a_real, a_imag = (factor[..., :half_width], factor[..., half_width:])
    return jnp.concatenate(
        [x_real * a_real + x_imag * a_imag, x_imag * a_real - x_real * a_imag], axis=-1
    )


def phases(coords_in, side_len):
    centre = jnp.arange(side_len, dtype=jnp.float32) - side_len / 2
    angles = coords_in[..., None] * centre * (2.0 * math.pi / side_len)
    return (jnp.cos(angles), jnp.sin(angles))


def grid_blocks(visib_rows, coord_rows, beam_terms):
    row_count = visib_rows.shape[-1] // 2
    side_len = beam_terms.shape[-2]
    cos_u, sin_u = phases(coord_rows[..., :row_count], side_len)
    cos_v, sin_v = phases(coord_rows[..., row_count:], side_len)
    vis_real = visib_rows[..., :row_count, None]
    vis_imag = visib_rows[..., row_count:, None]
    weighted = jnp.concatenate(
        [vis_real * cos_v - vis_imag * sin_v, vis_real * sin_v + vis_imag * cos_v], axis=-1
    )
    first = jnp.einsum("krl,krc->klc", cos_u, weighted, precision=highest)
    second = jnp.einsum("krl,krc->klc", sin_u, weighted, precision=highest)
    image_part = (first + rotate(second)) * (1.0 / math.sqrt(row_count))
    image_part = complex_mul(image_part, beam_terms)
    table_real, table_imag = tables(side_len)
    left_side = jnp.einsum("al,klc->kac", table_real, image_part, precision=highest)
    left_side = left_side + rotate(
        jnp.einsum("al,klc->kac", table_imag, image_part, precision=highest)
    )
    right_side = jnp.concatenate(
        [
            jnp.concatenate([table_real, table_imag], 1),
            jnp.concatenate([-table_imag, table_real], 1),
        ],
        0,
    )
    return jnp.einsum("kac,cd->kad", left_side, right_side, precision=highest)


def degrid_blocks(windows, coord_rows, beam_terms):
    side_len = windows.shape[-2]
    row_count = coord_rows.shape[-1] // 2
    table_real, table_imag = tables(side_len)
    left_side = jnp.einsum("al,klc->kac", table_real, windows, precision=highest)
    left_side = left_side - rotate(
        jnp.einsum("al,klc->kac", table_imag, windows, precision=highest)
    )
    right_side = jnp.concatenate(
        [
            jnp.concatenate([table_real, -table_imag], 1),
            jnp.concatenate([table_imag, table_real], 1),
        ],
        0,
    )
    image_part = jnp.einsum("kac,cd->kad", left_side, right_side, precision=highest)
    image_part = conj_mul(image_part, beam_terms)
    cos_u, sin_u = phases(coord_rows[..., :row_count], side_len)
    cos_v, sin_v = phases(coord_rows[..., row_count:], side_len)
    first = jnp.einsum("krl,klc->krc", cos_u, image_part, precision=highest)
    second = jnp.einsum("krl,klc->krc", sin_u, image_part, precision=highest)
    along_rows = first - rotate(second)
    a_real = along_rows[..., :side_len]
    a_imag = along_rows[..., side_len:]
    real_part = jnp.sum(a_real * cos_v + a_imag * sin_v, axis=-1)
    imag_part = jnp.sum(a_imag * cos_v - a_real * sin_v, axis=-1)
    return jnp.concatenate([real_part, imag_part], axis=-1) * (1.0 / side_len)


def body(visib, coords, owner, offsets, stations, live, beams, taper):
    n_vert = lax.axis_size("vert")
    my_row = lax.axis_index("au")
    my_col = lax.axis_index("vert")
    signal = visib[0]
    places = coords[0]
    owners = owner[0]
    shifts_in = offsets[0]
    pair_ids = stations[0]
    beam_rows = beams[0]
    sig_width = signal.shape[1]
    held_slot = jnp.arange(NB, dtype=jnp.int32)
    is_alive = held_slot < live[0, 0]
    heading = (owners // n_vert - my_row + 1) * 3 + (owners % n_vert - my_col + 1)
    heading = jnp.where(is_alive, heading, 4)
    order_in = jnp.sum(
        ((heading[:, None] == heading[None, :]) & (held_slot[None, :] < held_slot[:, None])).astype(
            jnp.int32
        ),
        axis=1,
    )
    route_ids = jnp.arange(9, dtype=jnp.int32)
    cap_slots = jnp.arange(CAP, dtype=jnp.int32)
    route_hit = (heading[None, None, :] == route_ids[:, None, None]) & (
        order_in[None, None, :] == cap_slots[None, :, None]
    )
    picked = jnp.sum(jnp.where(route_hit, held_slot[None, None, :], 0), axis=2)
    filled = jnp.any(route_hit, axis=2).astype(jnp.int32)
    row_data = jnp.concatenate([signal, places], axis=1)
    int_rows = jnp.concatenate([shifts_in, pair_ids], axis=1)
    send_floats = jnp.take(row_data, picked, axis=0) * filled[..., None].astype(jnp.float32)
    send_ints = jnp.concatenate([jnp.take(int_rows, picked, axis=0), filled[..., None]], axis=-1)
    int_width = send_ints.shape[-1]
    send_all = jnp.concatenate([send_floats, send_ints.astype(jnp.float32)], axis=-1)
    self_mask = (is_alive & (heading == 4)).astype(jnp.int32)
    float_parts = [row_data * self_mask[:, None].astype(jnp.float32)]
    int_parts = [jnp.concatenate([int_rows, self_mask[:, None]], axis=1)]
    for route_id in range(9):
        if route_id != 4:
            move_by = (route_id // 3 - 1) * n_vert + (route_id % 3 - 1)
            arrived = shifted(send_all[route_id], ("au", "vert"), move_by)
            float_parts.append(arrived[:, : 2 * sig_width])
            int_parts.append(arrived[:, 2 * sig_width :].astype(jnp.int32))
    slot_floats = jnp.concatenate(float_parts, axis=0)
    slot_ints = jnp.concatenate(int_parts, axis=0)
    slot_count = slot_floats.shape[0]
    slot_signal = slot_floats[:, :sig_width]
    slot_places = slot_floats[:, sig_width : 2 * sig_width]
    present = slot_ints[:, 4].astype(jnp.float32)
    wanted_ids = jnp.concatenate([slot_ints[:, 2], slot_ints[:, 3]], axis=0)
    piece_rows = lax.all_gather(beam_rows, ("au", "vert"), axis=0, tiled=True)
    station_ids = jnp.arange(piece_rows.shape[0], dtype=jnp.int32)
    one_hot = (wanted_ids[:, None] == station_ids[None, :]).astype(jnp.bfloat16)
    found_rows = jnp.dot(one_hot, piece_rows, preferred_element_type=jnp.float32)
    beam_terms = conj_mul(
        found_rows[:slot_count].reshape(slot_count, S, 2 * S),
        found_rows[slot_count:].reshape(slot_count, S, 2 * S),
    )
    subgrids = grid_blocks(slot_signal, slot_places, beam_terms) * present[:, None, None]
    rows_at = slot_ints[:, 0]
    cols_at = slot_ints[:, 1]
    span = jnp.arange(S, dtype=jnp.int32)
    grid_pos = jnp.arange(TS, dtype=jnp.int32)
    row_hot = (grid_pos[None, None, :] == (rows_at[:, None, None] + span[None, :, None])).astype(
        jnp.float32
    )
    col_hot = (grid_pos[None, None, :] == (cols_at[:, None, None] + span[None, :, None])).astype(
        jnp.float32
    )
    sub4 = subgrids.reshape(slot_count, S, 2, S)
    placed_cols = jnp.einsum("kasc,kcj->ksaj", sub4, col_hot, precision=highest)
    tile_sum = jnp.einsum("kai,ksaj->sij", row_hot, placed_cols, precision=highest)
    model_grid = lax.psum(tile_sum, "af") * taper[None]

    row_idx = (rows_at[:, None] + span[None, :]).reshape(-1)
    picked_rows = jnp.take(model_grid, row_idx, axis=1, mode="clip").reshape(2, slot_count, S, TS)
    windows = jnp.einsum("skaj,kcj->kasc", picked_rows, col_hot, precision=highest)
    windows = windows.reshape(slot_count, S, 2 * S)
    guesses = degrid_blocks(windows, slot_places, beam_terms)
    own_guess = guesses[:NB]
    returned = []
    slot_at = NB
    for route_id in range(9):
        if route_id == 4:
            returned.append(jnp.zeros((CAP, guesses.shape[1]), jnp.float32))
        else:
            move_by = (route_id // 3 - 1) * n_vert + (route_id % 3 - 1)
            block_part = guesses[slot_at : slot_at + CAP]
            slot_at = slot_at + CAP
            returned.append(shifted(block_part, ("au", "vert"), -move_by))
    stacked = jnp.stack(returned, axis=0).reshape(9 * CAP, guesses.shape[1])
    lookup = heading * CAP + jnp.minimum(order_in, CAP - 1)
    remote = jnp.take(stacked, lookup, axis=0)
    result = jnp.where((heading == 4)[:, None], own_guess, remote) * is_alive[:, None].astype(
        jnp.float32
    )
    return (result[None], model_grid)


def solution(mesh):
    placed = (
        P("af", ("au", "vert"), None),
        P("af", ("au", "vert"), None),
        P("af", ("au", "vert")),
        P("af", ("au", "vert"), None),
        P("af", ("au", "vert"), None),
        P("af", ("au", "vert")),
        P("af", ("au", "vert"), None),
        P("au", "vert"),
    )
    return jax.shard_map(
        body,
        mesh=mesh,
        in_specs=placed,
        out_specs=(P("af", ("au", "vert"), None), P(None, "au", "vert")),
        check_vma=False,
    )
```

```python
import math

import jax
import jax.numpy as jnp
from jax import lax
from jax.sharding import PartitionSpec as P

S = 64
CAP = 2
NB = 16
TS = 512


highest = lax.Precision.HIGHEST
part_type = jnp.bfloat16


def shifted(value, axis, steps):
    count = lax.axis_size(axis)
    leading, last = (max(0, -steps), min(count, count - steps))
    return lax.ppermute(value, axis, [(source, source + steps) for source in range(leading, last)])


def tables(side_len):
    positions = jnp.arange(side_len, dtype=jnp.int32)
    wrapped = positions[:, None] * positions[None, :] % side_len
    angles = wrapped.astype(jnp.float32) * (2.0 * math.pi / side_len)
    scaling = 1.0 / math.sqrt(side_len)
    return (jnp.cos(angles) * scaling, -jnp.sin(angles) * scaling)


def rotate(values):
    half_width = values.shape[-1] // 2
    return jnp.concatenate([-values[..., half_width:], values[..., :half_width]], axis=-1)


def complex_mul(values, factor):
    half_width = values.shape[-1] // 2
    x_real, x_imag = (values[..., :half_width], values[..., half_width:])
    a_real, a_imag = (factor[..., :half_width], factor[..., half_width:])
    return jnp.concatenate(
        [x_real * a_real - x_imag * a_imag, x_real * a_imag + x_imag * a_real], axis=-1
    )


def conj_mul(values, factor):
    half_width = values.shape[-1] // 2
    x_real, x_imag = (values[..., :half_width], values[..., half_width:])
    a_real, a_imag = (factor[..., :half_width], factor[..., half_width:])
    return jnp.concatenate(
        [x_real * a_real + x_imag * a_imag, x_imag * a_real - x_real * a_imag], axis=-1
    )


def phases(coords_in, side_len):
    coarse_n = 8
    fine_n = side_len // coarse_n
    step = 2.0 * math.pi / side_len
    coarse = (jnp.arange(coarse_n, dtype=jnp.float32) * fine_n - side_len / 2)
    fine = jnp.arange(fine_n, dtype=jnp.float32)
    coarse_angles = coords_in[..., None] * coarse * step
    fine_angles = coords_in[..., None] * fine * step
    cos_c, sin_c = jnp.cos(coarse_angles)[..., :, None], jnp.sin(coarse_angles)[..., :, None]
    cos_f, sin_f = jnp.cos(fine_angles)[..., None, :], jnp.sin(fine_angles)[..., None, :]
    shape = coords_in.shape + (side_len,)
    cos_all = (cos_c * cos_f - sin_c * sin_f).reshape(shape)
    sin_all = (sin_c * cos_f + cos_c * sin_f).reshape(shape)
    return (cos_all, sin_all)


def phase_sets(coord_rows, side_len):
    row_count = coord_rows.shape[-1] // 2
    cos_u, sin_u = phases(coord_rows[..., :row_count], side_len)
    cos_v, sin_v = phases(coord_rows[..., row_count:], side_len)
    return lax.optimization_barrier((cos_u, sin_u, cos_v, sin_v))


def split_parts(values):
    high = lax.reduce_precision(values, exponent_bits=8, mantissa_bits=7)
    rest = values - high
    middle = lax.reduce_precision(rest, exponent_bits=8, mantissa_bits=7)
    low = rest - middle
    return jnp.stack([high, middle, low], axis=0).astype(part_type)


def grid_blocks(visib_rows, phase_rows, beam_terms):
    row_count = visib_rows.shape[-1] // 2
    side_len = beam_terms.shape[-2]
    cos_u, sin_u, cos_v, sin_v = phase_rows
    vis_real = visib_rows[..., :row_count, None]
    vis_imag = visib_rows[..., row_count:, None]
    weighted = jnp.concatenate(
        [vis_real * cos_v - vis_imag * sin_v, vis_real * sin_v + vis_imag * cos_v], axis=-1
    )
    first = jnp.einsum("krl,krc->klc", cos_u, weighted, precision=highest)
    second = jnp.einsum("krl,krc->klc", sin_u, weighted, precision=highest)
    image_part = (first + rotate(second)) * (1.0 / math.sqrt(row_count))
    image_part = complex_mul(image_part, beam_terms)
    table_real, table_imag = tables(side_len)
    left_side = jnp.einsum("al,klc->kac", table_real, image_part, precision=highest)
    left_side = left_side + rotate(
        jnp.einsum("al,klc->kac", table_imag, image_part, precision=highest)
    )
    right_side = jnp.concatenate(
        [
            jnp.concatenate([table_real, table_imag], 1),
            jnp.concatenate([-table_imag, table_real], 1),
        ],
        0,
    )
    return jnp.einsum("kac,cd->kad", left_side, right_side, precision=highest)


def degrid_blocks(windows, phase_rows, beam_terms):
    side_len = windows.shape[-2]
    table_real, table_imag = tables(side_len)
    left_side = jnp.einsum("al,klc->kac", table_real, windows, precision=highest)
    left_side = left_side - rotate(
        jnp.einsum("al,klc->kac", table_imag, windows, precision=highest)
    )
    right_side = jnp.concatenate(
        [
            jnp.concatenate([table_real, -table_imag], 1),
            jnp.concatenate([table_imag, table_real], 1),
        ],
        0,
    )
    image_part = jnp.einsum("kac,cd->kad", left_side, right_side, precision=highest)
    image_part = conj_mul(image_part, beam_terms)
    cos_u, sin_u, cos_v, sin_v = phase_rows
    first = jnp.einsum("krl,klc->krc", cos_u, image_part, precision=highest)
    second = jnp.einsum("krl,klc->krc", sin_u, image_part, precision=highest)
    along_rows = first - rotate(second)
    a_real = along_rows[..., :side_len]
    a_imag = along_rows[..., side_len:]
    real_part = jnp.sum(a_real * cos_v + a_imag * sin_v, axis=-1)
    imag_part = jnp.sum(a_imag * cos_v - a_real * sin_v, axis=-1)
    return jnp.concatenate([real_part, imag_part], axis=-1) * (1.0 / side_len)


def body(visib, coords, owner, offsets, stations, live, beams, taper):
    n_vert = lax.axis_size("vert")
    my_row = lax.axis_index("au")
    my_col = lax.axis_index("vert")
    signal = visib[0]
    places = coords[0]
    owners = owner[0]
    shifts_in = offsets[0]
    pair_ids = stations[0]
    beam_rows = beams[0]
    sig_width = signal.shape[1]
    held_slot = jnp.arange(NB, dtype=jnp.int32)
    is_alive = held_slot < live[0, 0]
    heading = (owners // n_vert - my_row + 1) * 3 + (owners % n_vert - my_col + 1)
    heading = jnp.where(is_alive, heading, 4)
    order_in = jnp.sum(
        ((heading[:, None] == heading[None, :]) & (held_slot[None, :] < held_slot[:, None])).astype(
            jnp.int32
        ),
        axis=1,
    )
    route_ids = jnp.arange(9, dtype=jnp.int32)
    cap_slots = jnp.arange(CAP, dtype=jnp.int32)
    route_hit = (heading[None, None, :] == route_ids[:, None, None]) & (
        order_in[None, None, :] == cap_slots[None, :, None]
    )
    picked = jnp.sum(jnp.where(route_hit, held_slot[None, None, :], 0), axis=2)
    filled = jnp.any(route_hit, axis=2).astype(jnp.int32)
    row_data = jnp.concatenate([signal, places], axis=1)
    int_rows = jnp.concatenate([shifts_in, pair_ids], axis=1)
    send_floats = jnp.take(row_data, picked, axis=0) * filled[..., None].astype(jnp.float32)
    send_ints = jnp.concatenate([jnp.take(int_rows, picked, axis=0), filled[..., None]], axis=-1)
    int_width = send_ints.shape[-1]
    send_all = jnp.concatenate([send_floats, send_ints.astype(jnp.float32)], axis=-1)
    self_mask = (is_alive & (heading == 4)).astype(jnp.int32)
    float_parts = [row_data * self_mask[:, None].astype(jnp.float32)]
    int_parts = [jnp.concatenate([int_rows, self_mask[:, None]], axis=1)]
    for route_id in range(9):
        if route_id != 4:
            move_by = (route_id // 3 - 1) * n_vert + (route_id % 3 - 1)
            arrived = shifted(send_all[route_id], ("au", "vert"), move_by)
            float_parts.append(arrived[:, : 2 * sig_width])
            int_parts.append(arrived[:, 2 * sig_width :].astype(jnp.int32))
    slot_floats = jnp.concatenate(float_parts, axis=0)
    slot_ints = jnp.concatenate(int_parts, axis=0)
    slot_count = slot_floats.shape[0]
    slot_signal = slot_floats[:, :sig_width]
    slot_places = slot_floats[:, sig_width : 2 * sig_width]
    present = slot_ints[:, 4].astype(jnp.float32)
    wanted_ids = jnp.concatenate([slot_ints[:, 2], slot_ints[:, 3]], axis=0)
    piece_rows = lax.all_gather(beam_rows, ("au", "vert"), axis=0, tiled=True)
    station_ids = jnp.arange(piece_rows.shape[0], dtype=jnp.int32)
    one_hot = (wanted_ids[:, None] == station_ids[None, :]).astype(jnp.bfloat16)
    found_rows = jnp.dot(one_hot, piece_rows, preferred_element_type=jnp.float32)
    beam_terms = conj_mul(
        found_rows[:slot_count].reshape(slot_count, S, 2 * S),
        found_rows[slot_count:].reshape(slot_count, S, 2 * S),
    )
    phase_rows = phase_sets(slot_places, S)
    subgrids = grid_blocks(slot_signal, phase_rows, beam_terms) * present[:, None, None]
    rows_at = slot_ints[:, 0]
    cols_at = slot_ints[:, 1]
    span = jnp.arange(S, dtype=jnp.int32)
    grid_pos = jnp.arange(TS, dtype=jnp.int32)
    row_hot = (grid_pos[None, None, :] == (rows_at[:, None, None] + span[None, :, None])).astype(
        jnp.float32
    )
    col_hot = (grid_pos[None, None, :] == (cols_at[:, None, None] + span[None, :, None])).astype(
        jnp.float32
    )
    row_bits = row_hot.astype(part_type)
    col_bits = col_hot.astype(part_type)
    sub4 = split_parts(subgrids.reshape(slot_count, S, 2, S))
    placed_cols = jnp.einsum(
        "pkasc,kcj->pksaj", sub4, col_bits, preferred_element_type=jnp.float32
    ).sum(axis=0)
    placed_parts = split_parts(placed_cols)
    tile_sum = jnp.einsum(
        "kai,pksaj->psij", row_bits, placed_parts, preferred_element_type=jnp.float32
    ).sum(axis=0)
    model_grid = lax.psum(tile_sum, "af") * taper[None]

    model_parts = split_parts(model_grid)
    picked_rows = jnp.einsum(
        "kai,psij->pskaj", row_bits, model_parts, preferred_element_type=jnp.float32
    ).sum(axis=0)
    row_parts = split_parts(picked_rows)
    windows = jnp.einsum(
        "pskaj,kcj->pkasc", row_parts, col_bits, preferred_element_type=jnp.float32
    ).sum(axis=0)
    windows = windows.reshape(slot_count, S, 2 * S)
    guesses = degrid_blocks(windows, phase_rows, beam_terms)
    own_guess = guesses[:NB]
    returned = []
    slot_at = NB
    for route_id in range(9):
        if route_id == 4:
            returned.append(jnp.zeros((CAP, guesses.shape[1]), jnp.float32))
        else:
            move_by = (route_id // 3 - 1) * n_vert + (route_id % 3 - 1)
            block_part = guesses[slot_at : slot_at + CAP]
            slot_at = slot_at + CAP
            returned.append(shifted(block_part, ("au", "vert"), -move_by))
    stacked = jnp.stack(returned, axis=0).reshape(9 * CAP, guesses.shape[1])
    lookup = heading * CAP + jnp.minimum(order_in, CAP - 1)
    remote = jnp.take(stacked, lookup, axis=0)
    result = jnp.where((heading == 4)[:, None], own_guess, remote) * is_alive[:, None].astype(
        jnp.float32
    )
    return (result[None], model_grid)


def solution(mesh):
    placed = (
        P("af", ("au", "vert"), None),
        P("af", ("au", "vert"), None),
        P("af", ("au", "vert")),
        P("af", ("au", "vert"), None),
        P("af", ("au", "vert"), None),
        P("af", ("au", "vert")),
        P("af", ("au", "vert"), None),
        P("au", "vert"),
    )
    return jax.shard_map(
        body,
        mesh=mesh,
        in_specs=placed,
        out_specs=(P("af", ("au", "vert"), None), P(None, "au", "vert")),
        check_vma=False,
    )
```

```python
import math

import jax
import jax.numpy as jnp
from jax import lax
from jax.sharding import PartitionSpec as P

S = 64
CAP = 2
NB = 16
TS = 512


highest = lax.Precision.HIGHEST
high = lax.Precision.HIGH
part_type = jnp.bfloat16


def shifted(value, axis, steps):
    count = lax.axis_size(axis)
    leading, last = (max(0, -steps), min(count, count - steps))
    return lax.ppermute(value, axis, [(source, source + steps) for source in range(leading, last)])


def tables(side_len):
    positions = jnp.arange(side_len, dtype=jnp.int32)
    wrapped = positions[:, None] * positions[None, :] % side_len
    angles = wrapped.astype(jnp.float32) * (2.0 * math.pi / side_len)
    scaling = 1.0 / math.sqrt(side_len)
    return (jnp.cos(angles) * scaling, -jnp.sin(angles) * scaling)


def rotate(values):
    half_width = values.shape[-1] // 2
    return jnp.concatenate([-values[..., half_width:], values[..., :half_width]], axis=-1)


def complex_mul(values, factor):
    half_width = values.shape[-1] // 2
    x_real, x_imag = (values[..., :half_width], values[..., half_width:])
    a_real, a_imag = (factor[..., :half_width], factor[..., half_width:])
    return jnp.concatenate(
        [x_real * a_real - x_imag * a_imag, x_real * a_imag + x_imag * a_real], axis=-1
    )


def conj_mul(values, factor):
    half_width = values.shape[-1] // 2
    x_real, x_imag = (values[..., :half_width], values[..., half_width:])
    a_real, a_imag = (factor[..., :half_width], factor[..., half_width:])
    return jnp.concatenate(
        [x_real * a_real + x_imag * a_imag, x_imag * a_real - x_real * a_imag], axis=-1
    )


def phases(coords_in, side_len):
    coarse_n = 8
    fine_n = side_len // coarse_n
    step = 2.0 * math.pi / side_len
    coarse = (jnp.arange(coarse_n, dtype=jnp.float32) * fine_n - side_len / 2)
    fine = jnp.arange(fine_n, dtype=jnp.float32)
    coarse_angles = coords_in[..., None] * coarse * step
    fine_angles = coords_in[..., None] * fine * step
    cos_c, sin_c = jnp.cos(coarse_angles)[..., :, None], jnp.sin(coarse_angles)[..., :, None]
    cos_f, sin_f = jnp.cos(fine_angles)[..., None, :], jnp.sin(fine_angles)[..., None, :]
    shape = coords_in.shape + (side_len,)
    cos_all = (cos_c * cos_f - sin_c * sin_f).reshape(shape)
    sin_all = (sin_c * cos_f + cos_c * sin_f).reshape(shape)
    return (cos_all, sin_all)


def phase_sets(coord_rows, side_len):
    row_count = coord_rows.shape[-1] // 2
    cos_u, sin_u = phases(coord_rows[..., :row_count], side_len)
    cos_v, sin_v = phases(coord_rows[..., row_count:], side_len)
    return lax.optimization_barrier((cos_u, sin_u, cos_v, sin_v))


def split_parts(values):
    high = lax.reduce_precision(values, exponent_bits=8, mantissa_bits=7)
    rest = values - high
    middle = lax.reduce_precision(rest, exponent_bits=8, mantissa_bits=7)
    low = rest - middle
    return jnp.stack([high, middle, low], axis=0).astype(part_type)


def grid_blocks(visib_rows, phase_rows, beam_terms):
    row_count = visib_rows.shape[-1] // 2
    side_len = beam_terms.shape[-2]
    cos_u, sin_u, cos_v, sin_v = phase_rows
    vis_real = visib_rows[..., :row_count, None]
    vis_imag = visib_rows[..., row_count:, None]
    weighted = jnp.concatenate(
        [vis_real * cos_v - vis_imag * sin_v, vis_real * sin_v + vis_imag * cos_v], axis=-1
    )
    first = jnp.einsum("krl,krc->klc", cos_u, weighted, precision=high)
    second = jnp.einsum("krl,krc->klc", sin_u, weighted, precision=high)
    image_part = (first + rotate(second)) * (1.0 / math.sqrt(row_count))
    image_part = complex_mul(image_part, beam_terms)
    table_real, table_imag = tables(side_len)
    left_side = jnp.einsum("al,klc->kac", table_real, image_part, precision=high)
    left_side = left_side + rotate(
        jnp.einsum("al,klc->kac", table_imag, image_part, precision=high)
    )
    right_side = jnp.concatenate(
        [
            jnp.concatenate([table_real, table_imag], 1),
            jnp.concatenate([-table_imag, table_real], 1),
        ],
        0,
    )
    return jnp.einsum("kac,cd->kad", left_side, right_side, precision=high)


def degrid_blocks(windows, phase_rows, beam_terms):
    side_len = windows.shape[-2]
    table_real, table_imag = tables(side_len)
    left_side = jnp.einsum("al,klc->kac", table_real, windows, precision=high)
    left_side = left_side - rotate(
        jnp.einsum("al,klc->kac", table_imag, windows, precision=high)
    )
    right_side = jnp.concatenate(
        [
            jnp.concatenate([table_real, -table_imag], 1),
            jnp.concatenate([table_imag, table_real], 1),
        ],
        0,
    )
    image_part = jnp.einsum("kac,cd->kad", left_side, right_side, precision=high)
    image_part = conj_mul(image_part, beam_terms)
    cos_u, sin_u, cos_v, sin_v = phase_rows
    first = jnp.einsum("krl,klc->krc", cos_u, image_part, precision=high)
    second = jnp.einsum("krl,klc->krc", sin_u, image_part, precision=high)
    along_rows = first - rotate(second)
    a_real = along_rows[..., :side_len]
    a_imag = along_rows[..., side_len:]
    real_part = jnp.sum(a_real * cos_v + a_imag * sin_v, axis=-1)
    imag_part = jnp.sum(a_imag * cos_v - a_real * sin_v, axis=-1)
    return jnp.concatenate([real_part, imag_part], axis=-1) * (1.0 / side_len)


def body(visib, coords, owner, offsets, stations, live, beams, taper):
    n_vert = lax.axis_size("vert")
    my_row = lax.axis_index("au")
    my_col = lax.axis_index("vert")
    signal = visib[0]
    places = coords[0]
    owners = owner[0]
    shifts_in = offsets[0]
    pair_ids = stations[0]
    beam_rows = beams[0]
    sig_width = signal.shape[1]
    held_slot = jnp.arange(NB, dtype=jnp.int32)
    is_alive = held_slot < live[0, 0]
    heading = (owners // n_vert - my_row + 1) * 3 + (owners % n_vert - my_col + 1)
    heading = jnp.where(is_alive, heading, 4)
    order_in = jnp.sum(
        ((heading[:, None] == heading[None, :]) & (held_slot[None, :] < held_slot[:, None])).astype(
            jnp.int32
        ),
        axis=1,
    )
    route_ids = jnp.arange(9, dtype=jnp.int32)
    cap_slots = jnp.arange(CAP, dtype=jnp.int32)
    route_hit = (heading[None, None, :] == route_ids[:, None, None]) & (
        order_in[None, None, :] == cap_slots[None, :, None]
    )
    picked = jnp.sum(jnp.where(route_hit, held_slot[None, None, :], 0), axis=2)
    filled = jnp.any(route_hit, axis=2).astype(jnp.int32)
    row_data = jnp.concatenate([signal, places], axis=1)
    int_rows = jnp.concatenate([shifts_in, pair_ids], axis=1)
    send_floats = jnp.take(row_data, picked, axis=0) * filled[..., None].astype(jnp.float32)
    send_ints = jnp.concatenate([jnp.take(int_rows, picked, axis=0), filled[..., None]], axis=-1)
    int_width = send_ints.shape[-1]
    send_all = jnp.concatenate([send_floats, send_ints.astype(jnp.float32)], axis=-1)
    self_mask = (is_alive & (heading == 4)).astype(jnp.int32)
    float_parts = [row_data * self_mask[:, None].astype(jnp.float32)]
    int_parts = [jnp.concatenate([int_rows, self_mask[:, None]], axis=1)]
    for route_id in range(9):
        if route_id != 4:
            move_by = (route_id // 3 - 1) * n_vert + (route_id % 3 - 1)
            arrived = shifted(send_all[route_id], ("au", "vert"), move_by)
            float_parts.append(arrived[:, : 2 * sig_width])
            int_parts.append(arrived[:, 2 * sig_width :].astype(jnp.int32))
    slot_floats = jnp.concatenate(float_parts, axis=0)
    slot_ints = jnp.concatenate(int_parts, axis=0)
    slot_count = slot_floats.shape[0]
    slot_signal = slot_floats[:, :sig_width]
    slot_places = slot_floats[:, sig_width : 2 * sig_width]
    present = slot_ints[:, 4].astype(jnp.float32)
    wanted_ids = jnp.concatenate([slot_ints[:, 2], slot_ints[:, 3]], axis=0)
    piece_rows = lax.all_gather(beam_rows, ("au", "vert"), axis=0, tiled=True)
    station_ids = jnp.arange(piece_rows.shape[0], dtype=jnp.int32)
    one_hot = (wanted_ids[:, None] == station_ids[None, :]).astype(jnp.bfloat16)
    found_rows = jnp.dot(one_hot, piece_rows, preferred_element_type=jnp.float32)
    beam_terms = conj_mul(
        found_rows[:slot_count].reshape(slot_count, S, 2 * S),
        found_rows[slot_count:].reshape(slot_count, S, 2 * S),
    )
    phase_rows = phase_sets(slot_places, S)
    subgrids = grid_blocks(slot_signal, phase_rows, beam_terms) * present[:, None, None]
    rows_at = slot_ints[:, 0]
    cols_at = slot_ints[:, 1]
    span = jnp.arange(S, dtype=jnp.int32)
    grid_pos = jnp.arange(TS, dtype=jnp.int32)
    row_hot = (grid_pos[None, None, :] == (rows_at[:, None, None] + span[None, :, None])).astype(
        jnp.float32
    )
    col_hot = (grid_pos[None, None, :] == (cols_at[:, None, None] + span[None, :, None])).astype(
        jnp.float32
    )
    row_bits = row_hot.astype(part_type)
    col_bits = col_hot.astype(part_type)
    sub4 = split_parts(subgrids.reshape(slot_count, S, 2, S))
    placed_cols = jnp.einsum(
        "pkasc,kcj->pksaj", sub4, col_bits, preferred_element_type=jnp.float32
    ).sum(axis=0)
    placed_parts = split_parts(placed_cols)
    tile_sum = jnp.einsum(
        "kai,pksaj->psij", row_bits, placed_parts, preferred_element_type=jnp.float32
    ).sum(axis=0)
    model_grid = lax.psum(tile_sum, "af") * taper[None]

    model_parts = split_parts(model_grid)
    picked_rows = jnp.einsum(
        "kai,psij->pskaj", row_bits, model_parts, preferred_element_type=jnp.float32
    ).sum(axis=0)
    row_parts = split_parts(picked_rows)
    windows = jnp.einsum(
        "pskaj,kcj->pkasc", row_parts, col_bits, preferred_element_type=jnp.float32
    ).sum(axis=0)
    windows = windows.reshape(slot_count, S, 2 * S)
    far_guess = degrid_blocks(
        windows[NB:], tuple(rows[NB:] for rows in phase_rows), beam_terms[NB:]
    )
    own_guess = degrid_blocks(
        windows[:NB], tuple(rows[:NB] for rows in phase_rows), beam_terms[:NB]
    )
    guesses = jnp.concatenate([own_guess, far_guess], axis=0)
    returned = []
    slot_at = NB
    for route_id in range(9):
        if route_id == 4:
            returned.append(jnp.zeros((CAP, guesses.shape[1]), jnp.float32))
        else:
            move_by = (route_id // 3 - 1) * n_vert + (route_id % 3 - 1)
            block_part = guesses[slot_at : slot_at + CAP]
            slot_at = slot_at + CAP
            returned.append(shifted(block_part, ("au", "vert"), -move_by))
    stacked = jnp.stack(returned, axis=0).reshape(9 * CAP, guesses.shape[1])
    lookup = heading * CAP + jnp.minimum(order_in, CAP - 1)
    remote = jnp.take(stacked, lookup, axis=0)
    result = jnp.where((heading == 4)[:, None], own_guess, remote) * is_alive[:, None].astype(
        jnp.float32
    )
    return (result[None], model_grid)


def solution(mesh):
    placed = (
        P("af", ("au", "vert"), None),
        P("af", ("au", "vert"), None),
        P("af", ("au", "vert")),
        P("af", ("au", "vert"), None),
        P("af", ("au", "vert"), None),
        P("af", ("au", "vert")),
        P("af", ("au", "vert"), None),
        P("au", "vert"),
    )
    return jax.shard_map(
        body,
        mesh=mesh,
        in_specs=placed,
        out_specs=(P("af", ("au", "vert"), None), P(None, "au", "vert")),
        check_vma=False,
    )
```

```python
import math

import jax
import jax.numpy as jnp
from jax import lax
from jax.sharding import PartitionSpec as P

S = 64
CAP = 2
NB = 16
TS = 512


highest = lax.Precision.HIGHEST
high = lax.Precision.HIGH
part_type = jnp.bfloat16


def shifted(value, axis, steps):
    count = lax.axis_size(axis)
    leading, last = (max(0, -steps), min(count, count - steps))
    return lax.ppermute(value, axis, [(source, source + steps) for source in range(leading, last)])


def tables(side_len):
    positions = jnp.arange(side_len, dtype=jnp.int32)
    wrapped = positions[:, None] * positions[None, :] % side_len
    angles = wrapped.astype(jnp.float32) * (2.0 * math.pi / side_len)
    scaling = 1.0 / math.sqrt(side_len)
    return (jnp.cos(angles) * scaling, -jnp.sin(angles) * scaling)


def rotate(values):
    half_width = values.shape[-1] // 2
    return jnp.concatenate([-values[..., half_width:], values[..., :half_width]], axis=-1)


def complex_mul(values, factor):
    half_width = values.shape[-1] // 2
    x_real, x_imag = (values[..., :half_width], values[..., half_width:])
    a_real, a_imag = (factor[..., :half_width], factor[..., half_width:])
    return jnp.concatenate(
        [x_real * a_real - x_imag * a_imag, x_real * a_imag + x_imag * a_real], axis=-1
    )


def conj_mul(values, factor):
    half_width = values.shape[-1] // 2
    x_real, x_imag = (values[..., :half_width], values[..., half_width:])
    a_real, a_imag = (factor[..., :half_width], factor[..., half_width:])
    return jnp.concatenate(
        [x_real * a_real + x_imag * a_imag, x_imag * a_real - x_real * a_imag], axis=-1
    )


def phases(coords_in, side_len):
    coarse_n = 8
    fine_n = side_len // coarse_n
    step = 2.0 * math.pi / side_len
    coarse = (jnp.arange(coarse_n, dtype=jnp.float32) * fine_n - side_len / 2)
    fine = jnp.arange(fine_n, dtype=jnp.float32)
    coarse_angles = coords_in[..., None] * coarse * step
    fine_angles = coords_in[..., None] * fine * step
    cos_c, sin_c = jnp.cos(coarse_angles)[..., :, None], jnp.sin(coarse_angles)[..., :, None]
    cos_f, sin_f = jnp.cos(fine_angles)[..., None, :], jnp.sin(fine_angles)[..., None, :]
    shape = coords_in.shape + (side_len,)
    cos_all = (cos_c * cos_f - sin_c * sin_f).reshape(shape)
    sin_all = (sin_c * cos_f + cos_c * sin_f).reshape(shape)
    return (cos_all, sin_all)


def phase_sets(coord_rows, side_len):
    row_count = coord_rows.shape[-1] // 2
    cos_u, sin_u = phases(coord_rows[..., :row_count], side_len)
    cos_v, sin_v = phases(coord_rows[..., row_count:], side_len)
    return lax.optimization_barrier((cos_u, sin_u, cos_v, sin_v))


def split_parts(values):
    high = lax.reduce_precision(values, exponent_bits=8, mantissa_bits=7)
    rest = values - high
    middle = lax.reduce_precision(rest, exponent_bits=8, mantissa_bits=7)
    low = rest - middle
    return jnp.stack([high, middle, low], axis=0).astype(part_type)


def grid_blocks(visib_rows, phase_rows, beam_terms):
    row_count = visib_rows.shape[-1] // 2
    side_len = beam_terms.shape[-2]
    cos_u, sin_u, cos_v, sin_v = phase_rows
    vis_real = visib_rows[..., :row_count, None]
    vis_imag = visib_rows[..., row_count:, None]
    weighted = jnp.concatenate(
        [vis_real * cos_v - vis_imag * sin_v, vis_real * sin_v + vis_imag * cos_v], axis=-1
    )
    first = jnp.einsum("krl,krc->klc", cos_u, weighted, precision=high)
    second = jnp.einsum("krl,krc->klc", sin_u, weighted, precision=high)
    image_part = (first + rotate(second)) * (1.0 / math.sqrt(row_count))
    image_part = complex_mul(image_part, beam_terms)
    table_real, table_imag = tables(side_len)
    left_side = jnp.einsum("al,klc->kac", table_real, image_part, precision=high)
    left_side = left_side + rotate(
        jnp.einsum("al,klc->kac", table_imag, image_part, precision=high)
    )
    right_side = jnp.concatenate(
        [
            jnp.concatenate([table_real, table_imag], 1),
            jnp.concatenate([-table_imag, table_real], 1),
        ],
        0,
    )
    return jnp.einsum("kac,cd->kad", left_side, right_side, precision=high)


def degrid_blocks(windows, phase_rows, beam_terms):
    side_len = windows.shape[-2]
    table_real, table_imag = tables(side_len)
    left_side = jnp.einsum("al,klc->kac", table_real, windows, precision=high)
    left_side = left_side - rotate(
        jnp.einsum("al,klc->kac", table_imag, windows, precision=high)
    )
    right_side = jnp.concatenate(
        [
            jnp.concatenate([table_real, -table_imag], 1),
            jnp.concatenate([table_imag, table_real], 1),
        ],
        0,
    )
    image_part = jnp.einsum("kac,cd->kad", left_side, right_side, precision=high)
    image_part = conj_mul(image_part, beam_terms)
    cos_u, sin_u, cos_v, sin_v = phase_rows
    first = jnp.einsum("krl,klc->krc", cos_u, image_part, precision=high)
    second = jnp.einsum("krl,klc->krc", sin_u, image_part, precision=high)
    along_rows = first - rotate(second)
    a_real = along_rows[..., :side_len]
    a_imag = along_rows[..., side_len:]
    real_part = jnp.sum(a_real * cos_v + a_imag * sin_v, axis=-1)
    imag_part = jnp.sum(a_imag * cos_v - a_real * sin_v, axis=-1)
    return jnp.concatenate([real_part, imag_part], axis=-1) * (1.0 / side_len)


def body(visib, coords, owner, offsets, stations, live, beams, taper):
    n_vert = lax.axis_size("vert")
    my_row = lax.axis_index("au")
    my_col = lax.axis_index("vert")
    signal = visib[0]
    places = coords[0]
    owners = owner[0]
    shifts_in = offsets[0]
    pair_ids = stations[0]
    beam_rows = beams[0]
    sig_width = signal.shape[1]
    held_slot = jnp.arange(NB, dtype=jnp.int32)
    is_alive = held_slot < live[0, 0]
    heading = (owners // n_vert - my_row + 1) * 3 + (owners % n_vert - my_col + 1)
    heading = jnp.where(is_alive, heading, 4)
    order_in = jnp.sum(
        ((heading[:, None] == heading[None, :]) & (held_slot[None, :] < held_slot[:, None])).astype(
            jnp.int32
        ),
        axis=1,
    )
    route_ids = jnp.arange(9, dtype=jnp.int32)
    cap_slots = jnp.arange(CAP, dtype=jnp.int32)
    route_hit = (heading[None, None, :] == route_ids[:, None, None]) & (
        order_in[None, None, :] == cap_slots[None, :, None]
    )
    picked = jnp.sum(jnp.where(route_hit, held_slot[None, None, :], 0), axis=2)
    filled = jnp.any(route_hit, axis=2).astype(jnp.int32)
    row_data = jnp.concatenate([signal, places], axis=1)
    int_rows = jnp.concatenate([shifts_in, pair_ids], axis=1)
    send_floats = jnp.take(row_data, picked, axis=0) * filled[..., None].astype(jnp.float32)
    send_ints = jnp.concatenate([jnp.take(int_rows, picked, axis=0), filled[..., None]], axis=-1)
    int_width = send_ints.shape[-1]
    send_all = jnp.concatenate([send_floats, send_ints.astype(jnp.float32)], axis=-1)
    self_mask = (is_alive & (heading == 4)).astype(jnp.int32)
    float_parts = [row_data * self_mask[:, None].astype(jnp.float32)]
    int_parts = [jnp.concatenate([int_rows, self_mask[:, None]], axis=1)]
    for route_id in range(9):
        if route_id != 4:
            move_by = (route_id // 3 - 1) * n_vert + (route_id % 3 - 1)
            arrived = shifted(send_all[route_id], ("au", "vert"), move_by)
            float_parts.append(arrived[:, : 2 * sig_width])
            int_parts.append(arrived[:, 2 * sig_width :].astype(jnp.int32))
    slot_floats = jnp.concatenate(float_parts, axis=0)
    slot_ints = jnp.concatenate(int_parts, axis=0)
    slot_count = slot_floats.shape[0]
    slot_signal = slot_floats[:, :sig_width]
    slot_places = slot_floats[:, sig_width : 2 * sig_width]
    present = slot_ints[:, 4].astype(jnp.float32)
    wanted_ids = jnp.concatenate([slot_ints[:, 2], slot_ints[:, 3]], axis=0)
    piece_rows = lax.all_gather(beam_rows, ("au", "vert"), axis=0, tiled=True)
    station_ids = jnp.arange(piece_rows.shape[0], dtype=jnp.int32)
    one_hot = (wanted_ids[:, None] == station_ids[None, :]).astype(jnp.bfloat16)
    found_rows = jnp.dot(one_hot, piece_rows, preferred_element_type=jnp.float32)
    beam_terms = conj_mul(
        found_rows[:slot_count].reshape(slot_count, S, 2 * S),
        found_rows[slot_count:].reshape(slot_count, S, 2 * S),
    )
    phase_rows = phase_sets(slot_places, S)
    subgrids = grid_blocks(slot_signal, phase_rows, beam_terms) * present[:, None, None]
    rows_at = slot_ints[:, 0]
    cols_at = slot_ints[:, 1]
    span = jnp.arange(S, dtype=jnp.int32)
    grid_pos = jnp.arange(TS, dtype=jnp.int32)
    row_hot = (grid_pos[None, None, :] == (rows_at[:, None, None] + span[None, :, None])).astype(
        jnp.float32
    )
    col_hot = (grid_pos[None, None, :] == (cols_at[:, None, None] + span[None, :, None])).astype(
        jnp.float32
    )
    row_bits = row_hot.astype(part_type)
    col_bits = col_hot.astype(part_type)
    sub4 = split_parts(subgrids.reshape(slot_count, S, 2, S))
    placed_cols = jnp.einsum(
        "pkasc,kcj->pksaj", sub4, col_bits, preferred_element_type=jnp.float32
    ).sum(axis=0)
    placed_parts = split_parts(placed_cols)
    tile_sum = jnp.einsum(
        "kai,pksaj->psij", row_bits, placed_parts, preferred_element_type=jnp.float32
    ).sum(axis=0)
    model_grid = lax.psum(tile_sum, "af") * taper[None]

    model_parts = split_parts(model_grid)
    picked_rows = jnp.einsum(
        "kai,psij->pskaj", row_bits, model_parts, preferred_element_type=jnp.float32
    ).sum(axis=0)
    row_parts = split_parts(picked_rows)
    windows = jnp.einsum(
        "pskaj,kcj->pkasc", row_parts, col_bits, preferred_element_type=jnp.float32
    ).sum(axis=0)
    windows = windows.reshape(slot_count, S, 2 * S)
    far_guess = degrid_blocks(
        windows[NB:], tuple(rows[NB:] for rows in phase_rows), beam_terms[NB:]
    )
    own_guess = degrid_blocks(
        windows[:NB], tuple(rows[:NB] for rows in phase_rows), beam_terms[:NB]
    )
    guesses = jnp.concatenate([own_guess, far_guess], axis=0)
    route_moves = [
        (route_id // 3 - 1) * n_vert + (route_id % 3 - 1) for route_id in range(9) if route_id != 4
    ]
    holder_count = lax.axis_size(("au", "vert"))
    me = my_row * n_vert + my_col
    sent_parts = jnp.concatenate(
        [guesses[NB:].reshape(len(route_moves), CAP, -1), jnp.zeros((1, CAP, guesses.shape[1]))],
        axis=0,
    )
    peer_ids = jnp.arange(holder_count, dtype=jnp.int32)
    move_list = jnp.array(route_moves, dtype=jnp.int32)
    route_of_peer = jnp.sum(
        jnp.where(
            (me - move_list[None, :]) == peer_ids[:, None],
            jnp.arange(len(route_moves), dtype=jnp.int32)[None, :] + 1,
            0,
        ),
        axis=1,
    )
    route_of_peer = jnp.where(route_of_peer == 0, len(route_moves), route_of_peer - 1)
    send_buf = jnp.take(sent_parts, route_of_peer, axis=0)
    recv_buf = lax.all_to_all(send_buf, ("au", "vert"), 0, 0, tiled=True)
    from_peer = me + move_list
    peer_ok = (from_peer >= 0) & (from_peer < holder_count)
    arrived = jnp.take(recv_buf, jnp.clip(from_peer, 0, holder_count - 1), axis=0)
    arrived = arrived * peer_ok[:, None, None].astype(jnp.float32)
    returned = [arrived[i] for i in range(4)]
    returned.append(jnp.zeros((CAP, guesses.shape[1]), jnp.float32))
    returned.extend(arrived[i] for i in range(4, 8))
    stacked = jnp.stack(returned, axis=0).reshape(9 * CAP, guesses.shape[1])
    lookup = heading * CAP + jnp.minimum(order_in, CAP - 1)
    remote = jnp.take(stacked, lookup, axis=0)
    result = jnp.where((heading == 4)[:, None], own_guess, remote) * is_alive[:, None].astype(
        jnp.float32
    )
    return (result[None], model_grid)


def solution(mesh):
    placed = (
        P("af", ("au", "vert"), None),
        P("af", ("au", "vert"), None),
        P("af", ("au", "vert")),
        P("af", ("au", "vert"), None),
        P("af", ("au", "vert"), None),
        P("af", ("au", "vert")),
        P("af", ("au", "vert"), None),
        P("au", "vert"),
    )
    return jax.shard_map(
        body,
        mesh=mesh,
        in_specs=placed,
        out_specs=(P("af", ("au", "vert"), None), P(None, "au", "vert")),
        check_vma=False,
    )
```

```python
import math

import jax
import jax.numpy as jnp
from jax import lax
from jax.sharding import PartitionSpec as P

S = 64
CAP = 2
NB = 16
TS = 512


highest = lax.Precision.HIGHEST
high = lax.Precision.HIGH
part_type = jnp.bfloat16


def shifted(value, axis, steps):
    count = lax.axis_size(axis)
    leading, last = (max(0, -steps), min(count, count - steps))
    return lax.ppermute(value, axis, [(source, source + steps) for source in range(leading, last)])


def tables(side_len):
    positions = jnp.arange(side_len, dtype=jnp.int32)
    wrapped = positions[:, None] * positions[None, :] % side_len
    angles = wrapped.astype(jnp.float32) * (2.0 * math.pi / side_len)
    scaling = 1.0 / math.sqrt(side_len)
    return (jnp.cos(angles) * scaling, -jnp.sin(angles) * scaling)


def rotate(values):
    half_width = values.shape[-1] // 2
    return jnp.concatenate([-values[..., half_width:], values[..., :half_width]], axis=-1)


def complex_mul(values, factor):
    half_width = values.shape[-1] // 2
    x_real, x_imag = (values[..., :half_width], values[..., half_width:])
    a_real, a_imag = (factor[..., :half_width], factor[..., half_width:])
    return jnp.concatenate(
        [x_real * a_real - x_imag * a_imag, x_real * a_imag + x_imag * a_real], axis=-1
    )


def conj_mul(values, factor):
    half_width = values.shape[-1] // 2
    x_real, x_imag = (values[..., :half_width], values[..., half_width:])
    a_real, a_imag = (factor[..., :half_width], factor[..., half_width:])
    return jnp.concatenate(
        [x_real * a_real + x_imag * a_imag, x_imag * a_real - x_real * a_imag], axis=-1
    )


def phases(coords_in, side_len):
    coarse_n = 8
    fine_n = side_len // coarse_n
    step = 2.0 * math.pi / side_len
    coarse = (jnp.arange(coarse_n, dtype=jnp.float32) * fine_n - side_len / 2)
    fine = jnp.arange(fine_n, dtype=jnp.float32)
    coarse_angles = coords_in[..., None] * coarse * step
    fine_angles = coords_in[..., None] * fine * step
    cos_c, sin_c = jnp.cos(coarse_angles)[..., :, None], jnp.sin(coarse_angles)[..., :, None]
    cos_f, sin_f = jnp.cos(fine_angles)[..., None, :], jnp.sin(fine_angles)[..., None, :]
    shape = coords_in.shape + (side_len,)
    cos_all = (cos_c * cos_f - sin_c * sin_f).reshape(shape)
    sin_all = (sin_c * cos_f + cos_c * sin_f).reshape(shape)
    return (cos_all, sin_all)


def phase_sets(coord_rows, side_len):
    row_count = coord_rows.shape[-1] // 2
    cos_u, sin_u = phases(coord_rows[..., :row_count], side_len)
    cos_v, sin_v = phases(coord_rows[..., row_count:], side_len)
    return lax.optimization_barrier((cos_u, sin_u, cos_v, sin_v))


def split_parts(values):
    high = lax.reduce_precision(values, exponent_bits=8, mantissa_bits=7)
    rest = values - high
    return jnp.stack([high, rest], axis=0).astype(part_type)


def grid_blocks(visib_rows, phase_rows, beam_terms):
    row_count = visib_rows.shape[-1] // 2
    side_len = beam_terms.shape[-2]
    cos_u, sin_u, cos_v, sin_v = phase_rows
    vis_real = visib_rows[..., :row_count, None]
    vis_imag = visib_rows[..., row_count:, None]
    weighted = jnp.concatenate(
        [vis_real * cos_v - vis_imag * sin_v, vis_real * sin_v + vis_imag * cos_v], axis=-1
    )
    first = jnp.einsum("krl,krc->klc", cos_u, weighted, precision=high)
    second = jnp.einsum("krl,krc->klc", sin_u, weighted, precision=high)
    image_part = (first + rotate(second)) * (1.0 / math.sqrt(row_count))
    image_part = complex_mul(image_part, beam_terms)
    table_real, table_imag = tables(side_len)
    left_side = jnp.einsum("al,klc->kac", table_real, image_part, precision=high)
    left_side = left_side + rotate(
        jnp.einsum("al,klc->kac", table_imag, image_part, precision=high)
    )
    right_side = jnp.concatenate(
        [
            jnp.concatenate([table_real, table_imag], 1),
            jnp.concatenate([-table_imag, table_real], 1),
        ],
        0,
    )
    return jnp.einsum("kac,cd->kad", left_side, right_side, precision=high)


def degrid_blocks(windows, phase_rows, beam_terms):
    side_len = windows.shape[-2]
    table_real, table_imag = tables(side_len)
    left_side = jnp.einsum("al,klc->kac", table_real, windows, precision=high)
    left_side = left_side - rotate(
        jnp.einsum("al,klc->kac", table_imag, windows, precision=high)
    )
    right_side = jnp.concatenate(
        [
            jnp.concatenate([table_real, -table_imag], 1),
            jnp.concatenate([table_imag, table_real], 1),
        ],
        0,
    )
    image_part = jnp.einsum("kac,cd->kad", left_side, right_side, precision=high)
    image_part = conj_mul(image_part, beam_terms)
    cos_u, sin_u, cos_v, sin_v = phase_rows
    first = jnp.einsum("krl,klc->krc", cos_u, image_part, precision=high)
    second = jnp.einsum("krl,klc->krc", sin_u, image_part, precision=high)
    along_rows = first - rotate(second)
    a_real = along_rows[..., :side_len]
    a_imag = along_rows[..., side_len:]
    real_part = jnp.sum(a_real * cos_v + a_imag * sin_v, axis=-1)
    imag_part = jnp.sum(a_imag * cos_v - a_real * sin_v, axis=-1)
    return jnp.concatenate([real_part, imag_part], axis=-1) * (1.0 / side_len)


def body(visib, coords, owner, offsets, stations, live, beams, taper):
    n_vert = lax.axis_size("vert")
    my_row = lax.axis_index("au")
    my_col = lax.axis_index("vert")
    signal = visib[0]
    places = coords[0]
    owners = owner[0]
    shifts_in = offsets[0]
    pair_ids = stations[0]
    beam_rows = beams[0]
    sig_width = signal.shape[1]
    held_slot = jnp.arange(NB, dtype=jnp.int32)
    is_alive = held_slot < live[0, 0]
    heading = (owners // n_vert - my_row + 1) * 3 + (owners % n_vert - my_col + 1)
    heading = jnp.where(is_alive, heading, 4)
    order_in = jnp.sum(
        ((heading[:, None] == heading[None, :]) & (held_slot[None, :] < held_slot[:, None])).astype(
            jnp.int32
        ),
        axis=1,
    )
    route_ids = jnp.arange(9, dtype=jnp.int32)
    cap_slots = jnp.arange(CAP, dtype=jnp.int32)
    route_hit = (heading[None, None, :] == route_ids[:, None, None]) & (
        order_in[None, None, :] == cap_slots[None, :, None]
    )
    picked = jnp.sum(jnp.where(route_hit, held_slot[None, None, :], 0), axis=2)
    filled = jnp.any(route_hit, axis=2).astype(jnp.int32)
    row_data = jnp.concatenate([signal, places], axis=1)
    int_rows = jnp.concatenate([shifts_in, pair_ids], axis=1)
    send_floats = jnp.take(row_data, picked, axis=0) * filled[..., None].astype(jnp.float32)
    send_ints = jnp.concatenate([jnp.take(int_rows, picked, axis=0), filled[..., None]], axis=-1)
    int_width = send_ints.shape[-1]
    send_all = jnp.concatenate([send_floats, send_ints.astype(jnp.float32)], axis=-1)
    self_mask = (is_alive & (heading == 4)).astype(jnp.int32)
    float_parts = [row_data * self_mask[:, None].astype(jnp.float32)]
    int_parts = [jnp.concatenate([int_rows, self_mask[:, None]], axis=1)]
    for route_id in range(9):
        if route_id != 4:
            move_by = (route_id // 3 - 1) * n_vert + (route_id % 3 - 1)
            arrived = shifted(send_all[route_id], ("au", "vert"), move_by)
            float_parts.append(arrived[:, : 2 * sig_width])
            int_parts.append(arrived[:, 2 * sig_width :].astype(jnp.int32))
    slot_floats = jnp.concatenate(float_parts, axis=0)
    slot_ints = jnp.concatenate(int_parts, axis=0)
    slot_count = slot_floats.shape[0]
    slot_signal = slot_floats[:, :sig_width]
    slot_places = slot_floats[:, sig_width : 2 * sig_width]
    present = slot_ints[:, 4].astype(jnp.float32)
    wanted_ids = jnp.concatenate([slot_ints[:, 2], slot_ints[:, 3]], axis=0)
    piece_rows = lax.all_gather(beam_rows, ("au", "vert"), axis=0, tiled=True)
    station_ids = jnp.arange(piece_rows.shape[0], dtype=jnp.int32)
    one_hot = (wanted_ids[:, None] == station_ids[None, :]).astype(jnp.bfloat16)
    found_rows = jnp.dot(one_hot, piece_rows, preferred_element_type=jnp.float32)
    beam_terms = conj_mul(
        found_rows[:slot_count].reshape(slot_count, S, 2 * S),
        found_rows[slot_count:].reshape(slot_count, S, 2 * S),
    )
    phase_rows = phase_sets(slot_places, S)
    subgrids = grid_blocks(slot_signal, phase_rows, beam_terms) * present[:, None, None]
    rows_at = slot_ints[:, 0]
    cols_at = slot_ints[:, 1]
    span = jnp.arange(S, dtype=jnp.int32)
    grid_pos = jnp.arange(TS, dtype=jnp.int32)
    row_hot = (grid_pos[None, None, :] == (rows_at[:, None, None] + span[None, :, None])).astype(
        jnp.float32
    )
    col_hot = (grid_pos[None, None, :] == (cols_at[:, None, None] + span[None, :, None])).astype(
        jnp.float32
    )
    row_bits = row_hot.astype(part_type)
    col_bits = col_hot.astype(part_type)
    sub4 = split_parts(subgrids.reshape(slot_count, S, 2, S))
    placed_cols = jnp.einsum(
        "pkasc,kcj->pksaj", sub4, col_bits, preferred_element_type=jnp.float32
    ).sum(axis=0)
    placed_parts = split_parts(placed_cols)
    tile_sum = jnp.einsum(
        "kai,pksaj->psij", row_bits, placed_parts, preferred_element_type=jnp.float32
    ).sum(axis=0)
    model_grid = lax.psum(tile_sum, "af") * taper[None]

    model_parts = split_parts(model_grid)
    picked_rows = jnp.einsum(
        "kai,psij->pskaj", row_bits, model_parts, preferred_element_type=jnp.float32
    ).sum(axis=0)
    row_parts = split_parts(picked_rows)
    windows = jnp.einsum(
        "pskaj,kcj->pkasc", row_parts, col_bits, preferred_element_type=jnp.float32
    ).sum(axis=0)
    windows = windows.reshape(slot_count, S, 2 * S)
    far_guess = degrid_blocks(
        windows[NB:], tuple(rows[NB:] for rows in phase_rows), beam_terms[NB:]
    )
    own_guess = degrid_blocks(
        windows[:NB], tuple(rows[:NB] for rows in phase_rows), beam_terms[:NB]
    )
    guesses = jnp.concatenate([own_guess, far_guess], axis=0)
    route_moves = [
        (route_id // 3 - 1) * n_vert + (route_id % 3 - 1) for route_id in range(9) if route_id != 4
    ]
    holder_count = lax.axis_size(("au", "vert"))
    me = my_row * n_vert + my_col
    sent_parts = jnp.concatenate(
        [guesses[NB:].reshape(len(route_moves), CAP, -1), jnp.zeros((1, CAP, guesses.shape[1]))],
        axis=0,
    )
    peer_ids = jnp.arange(holder_count, dtype=jnp.int32)
    move_list = jnp.array(route_moves, dtype=jnp.int32)
    route_of_peer = jnp.sum(
        jnp.where(
            (me - move_list[None, :]) == peer_ids[:, None],
            jnp.arange(len(route_moves), dtype=jnp.int32)[None, :] + 1,
            0,
        ),
        axis=1,
    )
    route_of_peer = jnp.where(route_of_peer == 0, len(route_moves), route_of_peer - 1)
    send_buf = jnp.take(sent_parts, route_of_peer, axis=0)
    recv_buf = lax.all_to_all(send_buf, ("au", "vert"), 0, 0, tiled=True)
    from_peer = me + move_list
    peer_ok = (from_peer >= 0) & (from_peer < holder_count)
    arrived = jnp.take(recv_buf, jnp.clip(from_peer, 0, holder_count - 1), axis=0)
    arrived = arrived * peer_ok[:, None, None].astype(jnp.float32)
    returned = [arrived[i] for i in range(4)]
    returned.append(jnp.zeros((CAP, guesses.shape[1]), jnp.float32))
    returned.extend(arrived[i] for i in range(4, 8))
    stacked = jnp.stack(returned, axis=0).reshape(9 * CAP, guesses.shape[1])
    lookup = heading * CAP + jnp.minimum(order_in, CAP - 1)
    remote = jnp.take(stacked, lookup, axis=0)
    result = jnp.where((heading == 4)[:, None], own_guess, remote) * is_alive[:, None].astype(
        jnp.float32
    )
    return (result[None], model_grid)


def solution(mesh):
    placed = (
        P("af", ("au", "vert"), None),
        P("af", ("au", "vert"), None),
        P("af", ("au", "vert")),
        P("af", ("au", "vert"), None),
        P("af", ("au", "vert"), None),
        P("af", ("au", "vert")),
        P("af", ("au", "vert"), None),
        P("au", "vert"),
    )
    return jax.shard_map(
        body,
        mesh=mesh,
        in_specs=placed,
        out_specs=(P("af", ("au", "vert"), None), P(None, "au", "vert")),
        check_vma=False,
    )
```

```python
import math

import jax
import jax.numpy as jnp
from jax import lax
from jax.sharding import PartitionSpec as P

S = 64
CAP = 2
NB = 16
TS = 512


highest = lax.Precision.HIGHEST
high = lax.Precision.HIGH
part_type = jnp.bfloat16


def shifted(value, axis, steps):
    count = lax.axis_size(axis)
    leading, last = (max(0, -steps), min(count, count - steps))
    return lax.ppermute(value, axis, [(source, source + steps) for source in range(leading, last)])


def tables(side_len):
    positions = jnp.arange(side_len, dtype=jnp.int32)
    wrapped = positions[:, None] * positions[None, :] % side_len
    angles = wrapped.astype(jnp.float32) * (2.0 * math.pi / side_len)
    scaling = 1.0 / math.sqrt(side_len)
    return (jnp.cos(angles) * scaling, -jnp.sin(angles) * scaling)


def rotate(values):
    half_width = values.shape[-1] // 2
    return jnp.concatenate([-values[..., half_width:], values[..., :half_width]], axis=-1)


def complex_mul(values, factor):
    half_width = values.shape[-1] // 2
    x_real, x_imag = (values[..., :half_width], values[..., half_width:])
    a_real, a_imag = (factor[..., :half_width], factor[..., half_width:])
    return jnp.concatenate(
        [x_real * a_real - x_imag * a_imag, x_real * a_imag + x_imag * a_real], axis=-1
    )


def conj_mul(values, factor):
    half_width = values.shape[-1] // 2
    x_real, x_imag = (values[..., :half_width], values[..., half_width:])
    a_real, a_imag = (factor[..., :half_width], factor[..., half_width:])
    return jnp.concatenate(
        [x_real * a_real + x_imag * a_imag, x_imag * a_real - x_real * a_imag], axis=-1
    )


def phases(coords_in, side_len):
    coarse_n = 8
    fine_n = side_len // coarse_n
    step = 2.0 * math.pi / side_len
    coarse = (jnp.arange(coarse_n, dtype=jnp.float32) * fine_n - side_len / 2)
    fine = jnp.arange(fine_n, dtype=jnp.float32)
    coarse_angles = coords_in[..., None] * coarse * step
    fine_angles = coords_in[..., None] * fine * step
    cos_c, sin_c = jnp.cos(coarse_angles)[..., :, None], jnp.sin(coarse_angles)[..., :, None]
    cos_f, sin_f = jnp.cos(fine_angles)[..., None, :], jnp.sin(fine_angles)[..., None, :]
    shape = coords_in.shape + (side_len,)
    cos_all = (cos_c * cos_f - sin_c * sin_f).reshape(shape)
    sin_all = (sin_c * cos_f + cos_c * sin_f).reshape(shape)
    return (cos_all, sin_all)


def phase_sets(coord_rows, side_len):
    row_count = coord_rows.shape[-1] // 2
    cos_u, sin_u = phases(coord_rows[..., :row_count], side_len)
    cos_v, sin_v = phases(coord_rows[..., row_count:], side_len)
    return lax.optimization_barrier((cos_u, sin_u, cos_v, sin_v))


def split_parts(values):
    high = lax.reduce_precision(values, exponent_bits=8, mantissa_bits=7)
    rest = values - high
    middle = lax.reduce_precision(rest, exponent_bits=8, mantissa_bits=7)
    low = rest - middle
    return jnp.stack([high, middle, low], axis=0).astype(part_type)


def grid_blocks(visib_rows, phase_rows, beam_terms):
    row_count = visib_rows.shape[-1] // 2
    side_len = beam_terms.shape[-2]
    cos_u, sin_u, cos_v, sin_v = phase_rows
    vis_real = visib_rows[..., :row_count, None]
    vis_imag = visib_rows[..., row_count:, None]
    weighted = jnp.concatenate(
        [vis_real * cos_v - vis_imag * sin_v, vis_real * sin_v + vis_imag * cos_v], axis=-1
    )
    first = jnp.einsum("krl,krc->klc", cos_u, weighted, precision=high)
    second = jnp.einsum("krl,krc->klc", sin_u, weighted, precision=high)
    image_part = (first + rotate(second)) * (1.0 / math.sqrt(row_count))
    image_part = complex_mul(image_part, beam_terms)
    table_real, table_imag = tables(side_len)
    left_side = jnp.einsum("al,klc->kac", table_real, image_part, precision=high)
    left_side = left_side + rotate(
        jnp.einsum("al,klc->kac", table_imag, image_part, precision=high)
    )
    right_side = jnp.concatenate(
        [
            jnp.concatenate([table_real, table_imag], 1),
            jnp.concatenate([-table_imag, table_real], 1),
        ],
        0,
    )
    return jnp.einsum("kac,cd->kad", left_side, right_side, precision=high)


def degrid_blocks(windows, phase_rows, beam_terms):
    side_len = windows.shape[-2]
    table_real, table_imag = tables(side_len)
    left_side = jnp.einsum("al,klc->kac", table_real, windows, precision=high)
    left_side = left_side - rotate(
        jnp.einsum("al,klc->kac", table_imag, windows, precision=high)
    )
    right_side = jnp.concatenate(
        [
            jnp.concatenate([table_real, -table_imag], 1),
            jnp.concatenate([table_imag, table_real], 1),
        ],
        0,
    )
    image_part = jnp.einsum("kac,cd->kad", left_side, right_side, precision=high)
    image_part = conj_mul(image_part, beam_terms)
    cos_u, sin_u, cos_v, sin_v = phase_rows
    first = jnp.einsum("krl,klc->krc", cos_u, image_part, precision=high)
    second = jnp.einsum("krl,klc->krc", sin_u, image_part, precision=high)
    along_rows = first - rotate(second)
    a_real = along_rows[..., :side_len]
    a_imag = along_rows[..., side_len:]
    real_part = jnp.sum(a_real * cos_v + a_imag * sin_v, axis=-1)
    imag_part = jnp.sum(a_imag * cos_v - a_real * sin_v, axis=-1)
    return jnp.concatenate([real_part, imag_part], axis=-1) * (1.0 / side_len)


def body(visib, coords, owner, offsets, stations, live, beams, taper):
    n_vert = lax.axis_size("vert")
    my_row = lax.axis_index("au")
    my_col = lax.axis_index("vert")
    signal = visib[0]
    places = coords[0]
    owners = owner[0]
    shifts_in = offsets[0]
    pair_ids = stations[0]
    beam_rows = beams[0]
    sig_width = signal.shape[1]
    held_slot = jnp.arange(NB, dtype=jnp.int32)
    is_alive = held_slot < live[0, 0]
    heading = (owners // n_vert - my_row + 1) * 3 + (owners % n_vert - my_col + 1)
    heading = jnp.where(is_alive, heading, 4)
    order_in = jnp.sum(
        ((heading[:, None] == heading[None, :]) & (held_slot[None, :] < held_slot[:, None])).astype(
            jnp.int32
        ),
        axis=1,
    )
    route_ids = jnp.arange(9, dtype=jnp.int32)
    cap_slots = jnp.arange(CAP, dtype=jnp.int32)
    route_hit = (heading[None, None, :] == route_ids[:, None, None]) & (
        order_in[None, None, :] == cap_slots[None, :, None]
    )
    picked = jnp.sum(jnp.where(route_hit, held_slot[None, None, :], 0), axis=2)
    filled = jnp.any(route_hit, axis=2).astype(jnp.int32)
    row_data = jnp.concatenate([signal, places], axis=1)
    int_rows = jnp.concatenate([shifts_in, pair_ids], axis=1)
    send_floats = jnp.take(row_data, picked, axis=0) * filled[..., None].astype(jnp.float32)
    send_ints = jnp.concatenate([jnp.take(int_rows, picked, axis=0), filled[..., None]], axis=-1)
    int_width = send_ints.shape[-1]
    send_all = jnp.concatenate([send_floats, send_ints.astype(jnp.float32)], axis=-1)
    self_mask = (is_alive & (heading == 4)).astype(jnp.int32)
    float_parts = [row_data * self_mask[:, None].astype(jnp.float32)]
    int_parts = [jnp.concatenate([int_rows, self_mask[:, None]], axis=1)]
    holder_count = lax.axis_size(("au", "vert"))
    me = my_row * n_vert + my_col
    route_list = [route_id for route_id in range(9) if route_id != 4]
    route_moves = [(route_id // 3 - 1) * n_vert + (route_id % 3 - 1) for route_id in route_list]
    move_list = jnp.array(route_moves, dtype=jnp.int32)
    peer_ids = jnp.arange(holder_count, dtype=jnp.int32)
    route_slots = jnp.arange(len(route_moves), dtype=jnp.int32)

    def route_index(signed_moves):
        hit = (me + signed_moves[None, :]) == peer_ids[:, None]
        index = jnp.sum(jnp.where(hit, route_slots[None, :] + 1, 0), axis=1)
        return jnp.where(index == 0, len(route_moves), index - 1)

    outgoing = jnp.concatenate(
        [send_all[jnp.array(route_list)], jnp.zeros((1,) + send_all.shape[1:], jnp.float32)], axis=0
    )
    inbound = lax.all_to_all(
        jnp.take(outgoing, route_index(move_list), axis=0), ("au", "vert"), 0, 0, tiled=True
    )
    source_peer = me - move_list
    source_ok = (source_peer >= 0) & (source_peer < holder_count)
    landed = jnp.take(inbound, jnp.clip(source_peer, 0, holder_count - 1), axis=0)
    landed = landed * source_ok[:, None, None].astype(jnp.float32)
    for route_at in range(len(route_moves)):
        float_parts.append(landed[route_at, :, : 2 * sig_width])
        int_parts.append(landed[route_at, :, 2 * sig_width :].astype(jnp.int32))
    slot_floats = jnp.concatenate(float_parts, axis=0)
    slot_ints = jnp.concatenate(int_parts, axis=0)
    slot_count = slot_floats.shape[0]
    slot_signal = slot_floats[:, :sig_width]
    slot_places = slot_floats[:, sig_width : 2 * sig_width]
    present = slot_ints[:, 4].astype(jnp.float32)
    wanted_ids = jnp.concatenate([slot_ints[:, 2], slot_ints[:, 3]], axis=0)
    piece_rows = lax.all_gather(beam_rows, ("au", "vert"), axis=0, tiled=True)
    station_ids = jnp.arange(piece_rows.shape[0], dtype=jnp.int32)
    one_hot = (wanted_ids[:, None] == station_ids[None, :]).astype(jnp.bfloat16)
    found_rows = jnp.dot(one_hot, piece_rows, preferred_element_type=jnp.float32)
    beam_terms = conj_mul(
        found_rows[:slot_count].reshape(slot_count, S, 2 * S),
        found_rows[slot_count:].reshape(slot_count, S, 2 * S),
    )
    phase_rows = phase_sets(slot_places, S)
    subgrids = grid_blocks(slot_signal, phase_rows, beam_terms) * present[:, None, None]
    rows_at = slot_ints[:, 0]
    cols_at = slot_ints[:, 1]
    span = jnp.arange(S, dtype=jnp.int32)
    grid_pos = jnp.arange(TS, dtype=jnp.int32)
    row_hot = (grid_pos[None, None, :] == (rows_at[:, None, None] + span[None, :, None])).astype(
        jnp.float32
    )
    col_hot = (grid_pos[None, None, :] == (cols_at[:, None, None] + span[None, :, None])).astype(
        jnp.float32
    )
    row_bits = row_hot.astype(part_type)
    col_bits = col_hot.astype(part_type)
    sub4 = split_parts(subgrids.reshape(slot_count, S, 2, S))
    placed_cols = jnp.einsum(
        "pkasc,kcj->pksaj", sub4, col_bits, preferred_element_type=jnp.float32
    ).sum(axis=0)
    placed_parts = split_parts(placed_cols)
    tile_sum = jnp.einsum(
        "kai,pksaj->psij", row_bits, placed_parts, preferred_element_type=jnp.float32
    ).sum(axis=0)
    band = tile_sum.shape[1] // lax.axis_size("af")
    band_start = lax.axis_index("af") * band
    band_sum = lax.psum_scatter(tile_sum, "af", scatter_dimension=1, tiled=True)
    band_taper = lax.dynamic_slice_in_dim(taper, band_start, band, axis=0)
    model_grid = lax.all_gather(band_sum * band_taper[None], "af", axis=1, tiled=True)

    model_parts = split_parts(model_grid)
    picked_rows = jnp.einsum(
        "kai,psij->pskaj", row_bits, model_parts, preferred_element_type=jnp.float32
    ).sum(axis=0)
    row_parts = split_parts(picked_rows)
    windows = jnp.einsum(
        "pskaj,kcj->pkasc", row_parts, col_bits, preferred_element_type=jnp.float32
    ).sum(axis=0)
    windows = windows.reshape(slot_count, S, 2 * S)
    far_guess = degrid_blocks(
        windows[NB:], tuple(rows[NB:] for rows in phase_rows), beam_terms[NB:]
    )
    own_guess = degrid_blocks(
        windows[:NB], tuple(rows[:NB] for rows in phase_rows), beam_terms[:NB]
    )
    guesses = jnp.concatenate([own_guess, far_guess], axis=0)
    sent_parts = jnp.concatenate(
        [guesses[NB:].reshape(len(route_moves), CAP, -1), jnp.zeros((1, CAP, guesses.shape[1]))],
        axis=0,
    )
    route_of_peer = jnp.sum(
        jnp.where(
            (me - move_list[None, :]) == peer_ids[:, None],
            jnp.arange(len(route_moves), dtype=jnp.int32)[None, :] + 1,
            0,
        ),
        axis=1,
    )
    route_of_peer = jnp.where(route_of_peer == 0, len(route_moves), route_of_peer - 1)
    send_buf = jnp.take(sent_parts, route_of_peer, axis=0)
    recv_buf = lax.all_to_all(send_buf, ("au", "vert"), 0, 0, tiled=True)
    from_peer = me + move_list
    peer_ok = (from_peer >= 0) & (from_peer < holder_count)
    arrived = jnp.take(recv_buf, jnp.clip(from_peer, 0, holder_count - 1), axis=0)
    arrived = arrived * peer_ok[:, None, None].astype(jnp.float32)
    returned = [arrived[i] for i in range(4)]
    returned.append(jnp.zeros((CAP, guesses.shape[1]), jnp.float32))
    returned.extend(arrived[i] for i in range(4, 8))
    stacked = jnp.stack(returned, axis=0).reshape(9 * CAP, guesses.shape[1])
    lookup = heading * CAP + jnp.minimum(order_in, CAP - 1)
    remote = jnp.take(stacked, lookup, axis=0)
    result = jnp.where((heading == 4)[:, None], own_guess, remote) * is_alive[:, None].astype(
        jnp.float32
    )
    return (result[None], model_grid)


def solution(mesh):
    placed = (
        P("af", ("au", "vert"), None),
        P("af", ("au", "vert"), None),
        P("af", ("au", "vert")),
        P("af", ("au", "vert"), None),
        P("af", ("au", "vert"), None),
        P("af", ("au", "vert")),
        P("af", ("au", "vert"), None),
        P("au", "vert"),
    )
    return jax.shard_map(
        body,
        mesh=mesh,
        in_specs=placed,
        out_specs=(P("af", ("au", "vert"), None), P(None, "au", "vert")),
        check_vma=False,
    )
```

```python
import math

import jax
import jax.numpy as jnp
from jax import lax
from jax.sharding import PartitionSpec as P

S = 64
CAP = 2
NB = 16
TS = 512


highest = lax.Precision.HIGHEST
high = lax.Precision.HIGH
part_type = jnp.bfloat16


def shifted(value, axis, steps):
    count = lax.axis_size(axis)
    leading, last = (max(0, -steps), min(count, count - steps))
    return lax.ppermute(value, axis, [(source, source + steps) for source in range(leading, last)])


def tables(side_len):
    positions = jnp.arange(side_len, dtype=jnp.int32)
    wrapped = positions[:, None] * positions[None, :] % side_len
    angles = wrapped.astype(jnp.float32) * (2.0 * math.pi / side_len)
    scaling = 1.0 / math.sqrt(side_len)
    return (jnp.cos(angles) * scaling, -jnp.sin(angles) * scaling)


def rotate(values):
    half_width = values.shape[-1] // 2
    return jnp.concatenate([-values[..., half_width:], values[..., :half_width]], axis=-1)


def complex_mul(values, factor):
    half_width = values.shape[-1] // 2
    x_real, x_imag = (values[..., :half_width], values[..., half_width:])
    a_real, a_imag = (factor[..., :half_width], factor[..., half_width:])
    return jnp.concatenate(
        [x_real * a_real - x_imag * a_imag, x_real * a_imag + x_imag * a_real], axis=-1
    )


def conj_mul(values, factor):
    half_width = values.shape[-1] // 2
    x_real, x_imag = (values[..., :half_width], values[..., half_width:])
    a_real, a_imag = (factor[..., :half_width], factor[..., half_width:])
    return jnp.concatenate(
        [x_real * a_real + x_imag * a_imag, x_imag * a_real - x_real * a_imag], axis=-1
    )


def phases(coords_in, side_len):
    coarse_n = 8
    fine_n = side_len // coarse_n
    step = 2.0 * math.pi / side_len
    coarse = (jnp.arange(coarse_n, dtype=jnp.float32) * fine_n - side_len / 2)
    fine = jnp.arange(fine_n, dtype=jnp.float32)
    coarse_angles = coords_in[..., None] * coarse * step
    fine_angles = coords_in[..., None] * fine * step
    cos_c, sin_c = jnp.cos(coarse_angles)[..., :, None], jnp.sin(coarse_angles)[..., :, None]
    cos_f, sin_f = jnp.cos(fine_angles)[..., None, :], jnp.sin(fine_angles)[..., None, :]
    shape = coords_in.shape + (side_len,)
    cos_all = (cos_c * cos_f - sin_c * sin_f).reshape(shape)
    sin_all = (sin_c * cos_f + cos_c * sin_f).reshape(shape)
    return (cos_all, sin_all)


def phase_sets(coord_rows, side_len):
    row_count = coord_rows.shape[-1] // 2
    cos_u, sin_u = phases(coord_rows[..., :row_count], side_len)
    cos_v, sin_v = phases(coord_rows[..., row_count:], side_len)
    return lax.optimization_barrier((cos_u, sin_u, cos_v, sin_v))


def split_parts(values):
    high = lax.reduce_precision(values, exponent_bits=8, mantissa_bits=7)
    rest = values - high
    middle = lax.reduce_precision(rest, exponent_bits=8, mantissa_bits=7)
    low = rest - middle
    return jnp.stack([high, middle, low], axis=0).astype(part_type)


def grid_blocks(visib_rows, phase_rows, beam_terms):
    row_count = visib_rows.shape[-1] // 2
    side_len = beam_terms.shape[-2]
    cos_u, sin_u, cos_v, sin_v = phase_rows
    vis_real = visib_rows[..., :row_count, None]
    vis_imag = visib_rows[..., row_count:, None]
    weighted = jnp.concatenate(
        [vis_real * cos_v - vis_imag * sin_v, vis_real * sin_v + vis_imag * cos_v], axis=-1
    )
    first = jnp.einsum("krl,krc->klc", cos_u, weighted, precision=high)
    second = jnp.einsum("krl,krc->klc", sin_u, weighted, precision=high)
    image_part = (first + rotate(second)) * (1.0 / math.sqrt(row_count))
    image_part = complex_mul(image_part, beam_terms)
    table_real, table_imag = tables(side_len)
    left_side = jnp.einsum("al,klc->kac", table_real, image_part, precision=high)
    left_side = left_side + rotate(
        jnp.einsum("al,klc->kac", table_imag, image_part, precision=high)
    )
    right_side = jnp.concatenate(
        [
            jnp.concatenate([table_real, table_imag], 1),
            jnp.concatenate([-table_imag, table_real], 1),
        ],
        0,
    )
    return jnp.einsum("kac,cd->kad", left_side, right_side, precision=high)


def degrid_blocks(windows, phase_rows, beam_terms):
    side_len = windows.shape[-2]
    table_real, table_imag = tables(side_len)
    left_side = jnp.einsum("al,klc->kac", table_real, windows, precision=high)
    left_side = left_side - rotate(
        jnp.einsum("al,klc->kac", table_imag, windows, precision=high)
    )
    right_side = jnp.concatenate(
        [
            jnp.concatenate([table_real, -table_imag], 1),
            jnp.concatenate([table_imag, table_real], 1),
        ],
        0,
    )
    image_part = jnp.einsum("kac,cd->kad", left_side, right_side, precision=high)
    image_part = conj_mul(image_part, beam_terms)
    cos_u, sin_u, cos_v, sin_v = phase_rows
    first = jnp.einsum("krl,klc->krc", cos_u, image_part, precision=high)
    second = jnp.einsum("krl,klc->krc", sin_u, image_part, precision=high)
    along_rows = first - rotate(second)
    a_real = along_rows[..., :side_len]
    a_imag = along_rows[..., side_len:]
    real_part = jnp.sum(a_real * cos_v + a_imag * sin_v, axis=-1)
    imag_part = jnp.sum(a_imag * cos_v - a_real * sin_v, axis=-1)
    return jnp.concatenate([real_part, imag_part], axis=-1) * (1.0 / side_len)


def body(visib, coords, owner, offsets, stations, live, beams, taper):
    n_vert = lax.axis_size("vert")
    my_row = lax.axis_index("au")
    my_col = lax.axis_index("vert")
    signal = visib[0]
    places = coords[0]
    owners = owner[0]
    shifts_in = offsets[0]
    pair_ids = stations[0]
    beam_rows = beams[0]
    sig_width = signal.shape[1]
    held_slot = jnp.arange(NB, dtype=jnp.int32)
    is_alive = held_slot < live[0, 0]
    heading = (owners // n_vert - my_row + 1) * 3 + (owners % n_vert - my_col + 1)
    heading = jnp.where(is_alive, heading, 4)
    order_in = jnp.sum(
        ((heading[:, None] == heading[None, :]) & (held_slot[None, :] < held_slot[:, None])).astype(
            jnp.int32
        ),
        axis=1,
    )
    route_ids = jnp.arange(9, dtype=jnp.int32)
    cap_slots = jnp.arange(CAP, dtype=jnp.int32)
    route_hit = (heading[None, None, :] == route_ids[:, None, None]) & (
        order_in[None, None, :] == cap_slots[None, :, None]
    )
    picked = jnp.sum(jnp.where(route_hit, held_slot[None, None, :], 0), axis=2)
    filled = jnp.any(route_hit, axis=2).astype(jnp.int32)
    row_data = jnp.concatenate([signal, places], axis=1)
    int_rows = jnp.concatenate([shifts_in, pair_ids], axis=1)
    send_floats = jnp.take(row_data, picked, axis=0) * filled[..., None].astype(jnp.float32)
    send_ints = jnp.concatenate([jnp.take(int_rows, picked, axis=0), filled[..., None]], axis=-1)
    int_width = send_ints.shape[-1]
    send_all = jnp.concatenate([send_floats, send_ints.astype(jnp.float32)], axis=-1)
    self_mask = (is_alive & (heading == 4)).astype(jnp.int32)
    float_parts = [row_data * self_mask[:, None].astype(jnp.float32)]
    int_parts = [jnp.concatenate([int_rows, self_mask[:, None]], axis=1)]
    holder_count = lax.axis_size(("au", "vert"))
    me = my_row * n_vert + my_col
    route_list = [route_id for route_id in range(9) if route_id != 4]
    route_moves = [(route_id // 3 - 1) * n_vert + (route_id % 3 - 1) for route_id in route_list]
    move_list = jnp.array(route_moves, dtype=jnp.int32)
    peer_ids = jnp.arange(holder_count, dtype=jnp.int32)
    route_slots = jnp.arange(len(route_moves), dtype=jnp.int32)

    def route_index(signed_moves):
        hit = (me + signed_moves[None, :]) == peer_ids[:, None]
        index = jnp.sum(jnp.where(hit, route_slots[None, :] + 1, 0), axis=1)
        return jnp.where(index == 0, len(route_moves), index - 1)

    outgoing = jnp.concatenate(
        [send_all[jnp.array(route_list)], jnp.zeros((1,) + send_all.shape[1:], jnp.float32)], axis=0
    )
    inbound = lax.all_to_all(
        jnp.take(outgoing, route_index(move_list), axis=0), ("au", "vert"), 0, 0, tiled=True
    )
    source_peer = me - move_list
    source_ok = (source_peer >= 0) & (source_peer < holder_count)
    landed = jnp.take(inbound, jnp.clip(source_peer, 0, holder_count - 1), axis=0)
    landed = landed * source_ok[:, None, None].astype(jnp.float32)
    for route_at in range(len(route_moves)):
        float_parts.append(landed[route_at, :, : 2 * sig_width])
        int_parts.append(landed[route_at, :, 2 * sig_width :].astype(jnp.int32))
    slot_floats = jnp.concatenate(float_parts, axis=0)
    slot_ints = jnp.concatenate(int_parts, axis=0)
    slot_count = slot_floats.shape[0]
    slot_signal = slot_floats[:, :sig_width]
    slot_places = slot_floats[:, sig_width : 2 * sig_width]
    present = slot_ints[:, 4].astype(jnp.float32)
    wanted_ids = jnp.concatenate([slot_ints[:, 2], slot_ints[:, 3]], axis=0)
    piece_rows = lax.all_gather(beam_rows, ("au", "vert"), axis=0, tiled=True)
    station_ids = jnp.arange(piece_rows.shape[0], dtype=jnp.int32)
    one_hot = (wanted_ids[:, None] == station_ids[None, :]).astype(jnp.bfloat16)
    found_rows = jnp.dot(one_hot, piece_rows, preferred_element_type=jnp.float32)
    beam_terms = conj_mul(
        found_rows[:slot_count].reshape(slot_count, S, 2 * S),
        found_rows[slot_count:].reshape(slot_count, S, 2 * S),
    )
    phase_own = phase_sets(slot_places[:NB], S)
    phase_far = phase_sets(slot_places[NB:], S)
    subgrids = jnp.concatenate(
        [
            grid_blocks(slot_signal[:NB], phase_own, beam_terms[:NB]),
            grid_blocks(slot_signal[NB:], phase_far, beam_terms[NB:]),
        ],
        axis=0,
    ) * present[:, None, None]
    rows_at = slot_ints[:, 0]
    cols_at = slot_ints[:, 1]
    span = jnp.arange(S, dtype=jnp.int32)
    grid_pos = jnp.arange(TS, dtype=jnp.int32)
    row_hot = (grid_pos[None, None, :] == (rows_at[:, None, None] + span[None, :, None])).astype(
        jnp.float32
    )
    col_hot = (grid_pos[None, None, :] == (cols_at[:, None, None] + span[None, :, None])).astype(
        jnp.float32
    )
    row_bits = row_hot.astype(part_type)
    col_bits = col_hot.astype(part_type)
    sub4 = split_parts(subgrids.reshape(slot_count, S, 2, S))
    placed_cols = jnp.einsum(
        "pkasc,kcj->pksaj", sub4, col_bits, preferred_element_type=jnp.float32
    ).sum(axis=0)
    placed_parts = split_parts(placed_cols)
    tile_sum = jnp.einsum(
        "kai,pksaj->psij", row_bits, placed_parts, preferred_element_type=jnp.float32
    ).sum(axis=0)
    band = tile_sum.shape[1] // lax.axis_size("af")
    band_start = lax.axis_index("af") * band
    band_sum = lax.psum_scatter(tile_sum, "af", scatter_dimension=1, tiled=True)
    band_taper = lax.dynamic_slice_in_dim(taper, band_start, band, axis=0)
    model_grid = lax.all_gather(band_sum * band_taper[None], "af", axis=1, tiled=True)

    model_parts = split_parts(model_grid)
    picked_rows = jnp.einsum(
        "kai,psij->pskaj", row_bits, model_parts, preferred_element_type=jnp.float32
    ).sum(axis=0)
    row_parts = split_parts(picked_rows)
    windows = jnp.einsum(
        "pskaj,kcj->pkasc", row_parts, col_bits, preferred_element_type=jnp.float32
    ).sum(axis=0)
    windows = windows.reshape(slot_count, S, 2 * S)
    far_guess = degrid_blocks(windows[NB:], phase_far, beam_terms[NB:])
    own_guess = degrid_blocks(windows[:NB], phase_own, beam_terms[:NB])
    guesses = jnp.concatenate([own_guess, far_guess], axis=0)
    sent_parts = jnp.concatenate(
        [guesses[NB:].reshape(len(route_moves), CAP, -1), jnp.zeros((1, CAP, guesses.shape[1]))],
        axis=0,
    )
    route_of_peer = jnp.sum(
        jnp.where(
            (me - move_list[None, :]) == peer_ids[:, None],
            jnp.arange(len(route_moves), dtype=jnp.int32)[None, :] + 1,
            0,
        ),
        axis=1,
    )
    route_of_peer = jnp.where(route_of_peer == 0, len(route_moves), route_of_peer - 1)
    send_buf = jnp.take(sent_parts, route_of_peer, axis=0)
    recv_buf = lax.all_to_all(send_buf, ("au", "vert"), 0, 0, tiled=True)
    from_peer = me + move_list
    peer_ok = (from_peer >= 0) & (from_peer < holder_count)
    arrived = jnp.take(recv_buf, jnp.clip(from_peer, 0, holder_count - 1), axis=0)
    arrived = arrived * peer_ok[:, None, None].astype(jnp.float32)
    returned = [arrived[i] for i in range(4)]
    returned.append(jnp.zeros((CAP, guesses.shape[1]), jnp.float32))
    returned.extend(arrived[i] for i in range(4, 8))
    stacked = jnp.stack(returned, axis=0).reshape(9 * CAP, guesses.shape[1])
    lookup = heading * CAP + jnp.minimum(order_in, CAP - 1)
    remote = jnp.take(stacked, lookup, axis=0)
    result = jnp.where((heading == 4)[:, None], own_guess, remote) * is_alive[:, None].astype(
        jnp.float32
    )
    return (result[None], model_grid)


def solution(mesh):
    placed = (
        P("af", ("au", "vert"), None),
        P("af", ("au", "vert"), None),
        P("af", ("au", "vert")),
        P("af", ("au", "vert"), None),
        P("af", ("au", "vert"), None),
        P("af", ("au", "vert")),
        P("af", ("au", "vert"), None),
        P("au", "vert"),
    )
    return jax.shard_map(
        body,
        mesh=mesh,
        in_specs=placed,
        out_specs=(P("af", ("au", "vert"), None), P(None, "au", "vert")),
        check_vma=False,
    )
```

```python
import math

import jax
import jax.numpy as jnp
from jax import lax
from jax.sharding import PartitionSpec as P

S = 64
CAP = 2
NB = 16
TS = 512


highest = lax.Precision.HIGHEST
high = lax.Precision.HIGH
part_type = jnp.bfloat16


def shifted(value, axis, steps):
    count = lax.axis_size(axis)
    leading, last = (max(0, -steps), min(count, count - steps))
    return lax.ppermute(value, axis, [(source, source + steps) for source in range(leading, last)])


def tables(side_len):
    positions = jnp.arange(side_len, dtype=jnp.int32)
    wrapped = positions[:, None] * positions[None, :] % side_len
    angles = wrapped.astype(jnp.float32) * (2.0 * math.pi / side_len)
    scaling = 1.0 / math.sqrt(side_len)
    return (jnp.cos(angles) * scaling, -jnp.sin(angles) * scaling)


def rotate(values):
    half_width = values.shape[-1] // 2
    return jnp.concatenate([-values[..., half_width:], values[..., :half_width]], axis=-1)


def complex_mul(values, factor):
    half_width = values.shape[-1] // 2
    x_real, x_imag = (values[..., :half_width], values[..., half_width:])
    a_real, a_imag = (factor[..., :half_width], factor[..., half_width:])
    return jnp.concatenate(
        [x_real * a_real - x_imag * a_imag, x_real * a_imag + x_imag * a_real], axis=-1
    )


def conj_mul(values, factor):
    half_width = values.shape[-1] // 2
    x_real, x_imag = (values[..., :half_width], values[..., half_width:])
    a_real, a_imag = (factor[..., :half_width], factor[..., half_width:])
    return jnp.concatenate(
        [x_real * a_real + x_imag * a_imag, x_imag * a_real - x_real * a_imag], axis=-1
    )


def phases(coords_in, side_len):
    coarse_n = 8
    fine_n = side_len // coarse_n
    step = 2.0 * math.pi / side_len
    coarse = (jnp.arange(coarse_n, dtype=jnp.float32) * fine_n - side_len / 2)
    fine = jnp.arange(fine_n, dtype=jnp.float32)
    coarse_angles = coords_in[..., None] * coarse * step
    fine_angles = coords_in[..., None] * fine * step
    cos_c, sin_c = jnp.cos(coarse_angles)[..., :, None], jnp.sin(coarse_angles)[..., :, None]
    cos_f, sin_f = jnp.cos(fine_angles)[..., None, :], jnp.sin(fine_angles)[..., None, :]
    shape = coords_in.shape + (side_len,)
    cos_all = (cos_c * cos_f - sin_c * sin_f).reshape(shape)
    sin_all = (sin_c * cos_f + cos_c * sin_f).reshape(shape)
    return (cos_all, sin_all)


def phase_sets(coord_rows, side_len):
    row_count = coord_rows.shape[-1] // 2
    cos_u, sin_u = phases(coord_rows[..., :row_count], side_len)
    cos_v, sin_v = phases(coord_rows[..., row_count:], side_len)
    return lax.optimization_barrier((cos_u, sin_u, cos_v, sin_v))


def split_parts(values):
    high = lax.reduce_precision(values, exponent_bits=8, mantissa_bits=7)
    rest = values - high
    middle = lax.reduce_precision(rest, exponent_bits=8, mantissa_bits=7)
    low = rest - middle
    return jnp.stack([high, middle, low], axis=0).astype(part_type)


def grid_blocks(visib_rows, phase_rows, beam_terms):
    row_count = visib_rows.shape[-1] // 2
    side_len = beam_terms.shape[-2]
    cos_u, sin_u, cos_v, sin_v = phase_rows
    vis_real = visib_rows[..., :row_count, None]
    vis_imag = visib_rows[..., row_count:, None]
    weighted = jnp.concatenate(
        [vis_real * cos_v - vis_imag * sin_v, vis_real * sin_v + vis_imag * cos_v], axis=-1
    )
    first = jnp.einsum("krl,krc->klc", cos_u, weighted, precision=high)
    second = jnp.einsum("krl,krc->klc", sin_u, weighted, precision=high)
    image_part = (first + rotate(second)) * (1.0 / math.sqrt(row_count))
    image_part = complex_mul(image_part, beam_terms)
    table_real, table_imag = tables(side_len)
    left_side = jnp.einsum("al,klc->kac", table_real, image_part, precision=high)
    left_side = left_side + rotate(
        jnp.einsum("al,klc->kac", table_imag, image_part, precision=high)
    )
    right_side = jnp.concatenate(
        [
            jnp.concatenate([table_real, table_imag], 1),
            jnp.concatenate([-table_imag, table_real], 1),
        ],
        0,
    )
    return jnp.einsum("kac,cd->kad", left_side, right_side, precision=high)


def degrid_blocks(windows, phase_rows, beam_terms):
    side_len = windows.shape[-2]
    table_real, table_imag = tables(side_len)
    left_side = jnp.einsum("al,klc->kac", table_real, windows, precision=high)
    left_side = left_side - rotate(
        jnp.einsum("al,klc->kac", table_imag, windows, precision=high)
    )
    right_side = jnp.concatenate(
        [
            jnp.concatenate([table_real, -table_imag], 1),
            jnp.concatenate([table_imag, table_real], 1),
        ],
        0,
    )
    image_part = jnp.einsum("kac,cd->kad", left_side, right_side, precision=high)
    image_part = conj_mul(image_part, beam_terms)
    cos_u, sin_u, cos_v, sin_v = phase_rows
    first = jnp.einsum("krl,klc->krc", cos_u, image_part, precision=high)
    second = jnp.einsum("krl,klc->krc", sin_u, image_part, precision=high)
    along_rows = first - rotate(second)
    a_real = along_rows[..., :side_len]
    a_imag = along_rows[..., side_len:]
    real_part = jnp.sum(a_real * cos_v + a_imag * sin_v, axis=-1)
    imag_part = jnp.sum(a_imag * cos_v - a_real * sin_v, axis=-1)
    return jnp.concatenate([real_part, imag_part], axis=-1) * (1.0 / side_len)


def body(visib, coords, owner, offsets, stations, live, beams, taper):
    n_vert = lax.axis_size("vert")
    my_row = lax.axis_index("au")
    my_col = lax.axis_index("vert")
    signal = visib[0]
    places = coords[0]
    owners = owner[0]
    shifts_in = offsets[0]
    pair_ids = stations[0]
    beam_rows = beams[0]
    sig_width = signal.shape[1]
    held_slot = jnp.arange(NB, dtype=jnp.int32)
    is_alive = held_slot < live[0, 0]
    heading = (owners // n_vert - my_row + 1) * 3 + (owners % n_vert - my_col + 1)
    heading = jnp.where(is_alive, heading, 4)
    order_in = jnp.sum(
        ((heading[:, None] == heading[None, :]) & (held_slot[None, :] < held_slot[:, None])).astype(
            jnp.int32
        ),
        axis=1,
    )
    route_ids = jnp.arange(9, dtype=jnp.int32)
    cap_slots = jnp.arange(CAP, dtype=jnp.int32)
    route_hit = (heading[None, None, :] == route_ids[:, None, None]) & (
        order_in[None, None, :] == cap_slots[None, :, None]
    )
    picked = jnp.sum(jnp.where(route_hit, held_slot[None, None, :], 0), axis=2)
    filled = jnp.any(route_hit, axis=2).astype(jnp.int32)
    row_data = jnp.concatenate([signal, places], axis=1)
    int_rows = jnp.concatenate([shifts_in, pair_ids], axis=1)
    send_floats = jnp.take(row_data, picked, axis=0) * filled[..., None].astype(jnp.float32)
    send_ints = jnp.concatenate([jnp.take(int_rows, picked, axis=0), filled[..., None]], axis=-1)
    int_width = send_ints.shape[-1]
    send_all = jnp.concatenate([send_floats, send_ints.astype(jnp.float32)], axis=-1)
    self_mask = (is_alive & (heading == 4)).astype(jnp.int32)
    float_parts = [row_data * self_mask[:, None].astype(jnp.float32)]
    int_parts = [jnp.concatenate([int_rows, self_mask[:, None]], axis=1)]
    for route_id in range(9):
        if route_id != 4:
            move_by = (route_id // 3 - 1) * n_vert + (route_id % 3 - 1)
            arrived = shifted(send_all[route_id], ("au", "vert"), move_by)
            float_parts.append(arrived[:, : 2 * sig_width])
            int_parts.append(arrived[:, 2 * sig_width :].astype(jnp.int32))
    slot_floats = jnp.concatenate(float_parts, axis=0)
    slot_ints = jnp.concatenate(int_parts, axis=0)
    slot_count = slot_floats.shape[0]
    slot_signal = slot_floats[:, :sig_width]
    slot_places = slot_floats[:, sig_width : 2 * sig_width]
    present = slot_ints[:, 4].astype(jnp.float32)
    wanted_ids = jnp.concatenate([slot_ints[:, 2], slot_ints[:, 3]], axis=0)
    piece_rows = lax.all_gather(beam_rows, ("au", "vert"), axis=0, tiled=True)
    station_ids = jnp.arange(piece_rows.shape[0], dtype=jnp.int32)
    one_hot = (wanted_ids[:, None] == station_ids[None, :]).astype(jnp.bfloat16)
    found_rows = jnp.dot(one_hot, piece_rows, preferred_element_type=jnp.float32)
    beam_terms = conj_mul(
        found_rows[:slot_count].reshape(slot_count, S, 2 * S),
        found_rows[slot_count:].reshape(slot_count, S, 2 * S),
    )
    phase_rows = phase_sets(slot_places, S)
    subgrids = grid_blocks(slot_signal, phase_rows, beam_terms) * present[:, None, None]
    rows_at = slot_ints[:, 0]
    cols_at = slot_ints[:, 1]
    span = jnp.arange(S, dtype=jnp.int32)
    grid_pos = jnp.arange(TS, dtype=jnp.int32)
    row_hot = (grid_pos[None, None, :] == (rows_at[:, None, None] + span[None, :, None])).astype(
        jnp.float32
    )
    col_hot = (grid_pos[None, None, :] == (cols_at[:, None, None] + span[None, :, None])).astype(
        jnp.float32
    )
    row_bits = row_hot.astype(part_type)
    col_bits = col_hot.astype(part_type)
    sub4 = split_parts(subgrids.reshape(slot_count, S, 2, S))
    placed_cols = jnp.einsum(
        "pkasc,kcj->pksaj", sub4, col_bits, preferred_element_type=jnp.float32
    ).sum(axis=0)
    placed_parts = split_parts(placed_cols)
    tile_sum = jnp.einsum(
        "kai,pksaj->psij", row_bits, placed_parts, preferred_element_type=jnp.float32
    ).sum(axis=0)
    band = tile_sum.shape[1] // lax.axis_size("af")
    band_start = lax.axis_index("af") * band
    band_sum = lax.psum_scatter(tile_sum, "af", scatter_dimension=1, tiled=True)
    band_taper = lax.dynamic_slice_in_dim(taper, band_start, band, axis=0)
    model_grid = lax.all_gather(band_sum * band_taper[None], "af", axis=1, tiled=True)

    model_parts = split_parts(model_grid)
    picked_rows = jnp.einsum(
        "kai,psij->pskaj", row_bits, model_parts, preferred_element_type=jnp.float32
    ).sum(axis=0)
    row_parts = split_parts(picked_rows)
    windows = jnp.einsum(
        "pskaj,kcj->pkasc", row_parts, col_bits, preferred_element_type=jnp.float32
    ).sum(axis=0)
    windows = windows.reshape(slot_count, S, 2 * S)
    far_guess = degrid_blocks(
        windows[NB:], tuple(rows[NB:] for rows in phase_rows), beam_terms[NB:]
    )
    own_guess = degrid_blocks(
        windows[:NB], tuple(rows[:NB] for rows in phase_rows), beam_terms[:NB]
    )
    guesses = jnp.concatenate([own_guess, far_guess], axis=0)
    route_moves = [
        (route_id // 3 - 1) * n_vert + (route_id % 3 - 1) for route_id in range(9) if route_id != 4
    ]
    holder_count = lax.axis_size(("au", "vert"))
    me = my_row * n_vert + my_col
    sent_parts = jnp.concatenate(
        [guesses[NB:].reshape(len(route_moves), CAP, -1), jnp.zeros((1, CAP, guesses.shape[1]))],
        axis=0,
    )
    peer_ids = jnp.arange(holder_count, dtype=jnp.int32)
    move_list = jnp.array(route_moves, dtype=jnp.int32)
    route_of_peer = jnp.sum(
        jnp.where(
            (me - move_list[None, :]) == peer_ids[:, None],
            jnp.arange(len(route_moves), dtype=jnp.int32)[None, :] + 1,
            0,
        ),
        axis=1,
    )
    route_of_peer = jnp.where(route_of_peer == 0, len(route_moves), route_of_peer - 1)
    send_buf = jnp.take(sent_parts, route_of_peer, axis=0)
    recv_buf = lax.all_to_all(send_buf, ("au", "vert"), 0, 0, tiled=True)
    from_peer = me + move_list
    peer_ok = (from_peer >= 0) & (from_peer < holder_count)
    arrived = jnp.take(recv_buf, jnp.clip(from_peer, 0, holder_count - 1), axis=0)
    arrived = arrived * peer_ok[:, None, None].astype(jnp.float32)
    returned = [arrived[i] for i in range(4)]
    returned.append(jnp.zeros((CAP, guesses.shape[1]), jnp.float32))
    returned.extend(arrived[i] for i in range(4, 8))
    stacked = jnp.stack(returned, axis=0).reshape(9 * CAP, guesses.shape[1])
    lookup = heading * CAP + jnp.minimum(order_in, CAP - 1)
    remote = jnp.take(stacked, lookup, axis=0)
    result = jnp.where((heading == 4)[:, None], own_guess, remote) * is_alive[:, None].astype(
        jnp.float32
    )
    return (result[None], model_grid)


def solution(mesh):
    placed = (
        P("af", ("au", "vert"), None),
        P("af", ("au", "vert"), None),
        P("af", ("au", "vert")),
        P("af", ("au", "vert"), None),
        P("af", ("au", "vert"), None),
        P("af", ("au", "vert")),
        P("af", ("au", "vert"), None),
        P("au", "vert"),
    )
    return jax.shard_map(
        body,
        mesh=mesh,
        in_specs=placed,
        out_specs=(P("af", ("au", "vert"), None), P(None, "au", "vert")),
        check_vma=False,
    )
```
